512 devices in a mesh: grid: 64 (over x, z, core), orb: 8 (over y).
Axes of the slice: x: 4, y: 8, z: 8, core: 2. Of those that a mesh axis runs over, the one named last changes fastest.
Arguments:
- orbitals: float32 [256, 16, 16, 1024], P('grid', None, None, 'orb'), may hold values from -15 to 15
- potential: float32 [256, 16, 16], P('grid'), may hold values from -2 to 0
Outputs:
- filtered: float32 [256, 16, 16, 1024], P('grid', None, None, 'orb')
- hamiltonian_block: float32 [1024, 1024], P('orb', 'grid')
- margin_block: float32 [1024, 1024], P('orb', 'grid')
The draws below stay inside these ranges and needn't reach their ends.
All inputs are finite; a program needn't handle non-finite values.
Results may differ from the reference program's by a relative error of at most 0.0039.
Values may be sent and summed in bfloat16 or wider, within the bound.
No kernel may reach another device: no remote copies, remote signals or barrier semaphores. Data moves between devices by JAX's collectives and lax.ppermute only.
A program may use at most 64 MiB of HBM per device.

```python
import math
import jax
import jax.numpy as jnp
from jax import lax

NORB = 1024
DEGREE = 4
PY = 16
PX = 16
NZ = 256


def draw_orbitals(key, part):
    depth_frac = jnp.arange(NZ, dtype=jnp.float32) / max(NZ - 1, 1)
    envelope = jnp.exp(math.log(3.0) * depth_frac)[:, None, None, None]
    key_main = jax.random.fold_in(key, 0)
    gaussian = jnp.clip(jax.random.normal(key_main, (NZ, PY, PX, NORB), jnp.float32), -4.5, 4.5)
    return gaussian * envelope


def block_scale(stream_key, dims, shards, low, largest):
    def one(position, parts):
        heights = jax.random.uniform(jax.random.fold_in(jax.random.fold_in(stream_key, 6), position), (parts,), jnp.float32, low / len(shards), largest / len(shards))
        return jnp.repeat(jnp.exp(heights), dims[position] // parts).reshape((-1,) + (1,) * (len(dims) - position - 1))

    loudness = one(*shards[0])
    for cut in shards[1:]:
        loudness = loudness * one(*cut)
    return loudness


def setup_inputs(seed: int = 0) -> dict:
    splits = jax.random.split(jax.random.key(seed), 3)
    orbitals = draw_orbitals(jax.random.fold_in(splits[2], 71), 0)
    potential = jnp.clip(-2.0 + 2.0 * jax.random.uniform(splits[1], (NZ, PY, PX), jnp.float32) ** block_scale(splits[1], (NZ, PY, PX), ((0, 64),), -0.2, 0.2), -2.0, 0.0)
    return {"orbitals": orbitals, "potential": potential}


STENCIL = (-205.0 / 72.0, 8.0 / 5.0, -1.0 / 5.0, 8.0 / 315.0, -1.0 / 560.0)
LOWER_EDGE = -2.0
CUT_EDGE = 1.5
UPPER_EDGE = 10.0
EPSILON = 1e-06

def apply_hamiltonian(current, potential):
    layers = current.shape[0]
    padded = jnp.pad(current, ((4, 4), (0, 0), (0, 0), (0, 0)))
    laplacian = 3.0 * STENCIL[0] * current
    for offset in range(1, 5):
        laplacian = laplacian + STENCIL[offset] * (padded[4 + offset:4 + offset + layers] + padded[4 - offset:4 - offset + layers])
        laplacian = laplacian + STENCIL[offset] * (jnp.roll(current, offset, 1) + jnp.roll(current, -offset, 1) + jnp.roll(current, offset, 2) + jnp.roll(current, -offset, 2))
    return -0.5 * laplacian + potential[:, :, :, None] * current

def chebyshev(initial, potential):
    half_width = (UPPER_EDGE - CUT_EDGE) / 2.0
    centre = (UPPER_EDGE + CUT_EDGE) / 2.0
    sigma_now = half_width / (LOWER_EDGE - centre)
    gamma_ratio = 2.0 / sigma_now
    previous = initial
    current = sigma_now / half_width * (apply_hamiltonian(previous, potential) - centre * previous)
    for degree_step in range(DEGREE - 1):
        sigma_next = 1.0 / (gamma_ratio - sigma_now)
        following = 2.0 * sigma_next / half_width * (apply_hamiltonian(current, potential) - centre * current) - sigma_now * sigma_next * previous
        previous, current, sigma_now = (current, following, sigma_next)
    return current

def contract_points(left_side, right_side):
    return lax.dot_general(left_side.astype(jnp.float32), right_side.astype(jnp.float32), (((0,), (0,)), ((), ())), precision=lax.Precision.HIGHEST, preferred_element_type=jnp.float32)

def reference(orbitals, potential):
    block_width = min(256, NORB)
    point_total = NZ * PY * PX
    filtered_parts = []
    rounded_parts = []
    image_parts = []
    for block_index in range(NORB // block_width):
        initial = orbitals[:, :, :, block_index * block_width:(block_index + 1) * block_width]
        result_block = chebyshev(initial, potential)
        filtered_parts.append(result_block)
        rounded_parts.append(result_block.astype(jnp.bfloat16))
        image_parts.append(apply_hamiltonian(result_block, potential).astype(jnp.bfloat16))
    result_all = jnp.concatenate(filtered_parts, axis=3)
    squares = lax.optimization_barrier(jnp.sum(result_all * result_all, axis=(0, 1, 2)))
    scale_all = 1.0 / jnp.sqrt(squares / point_total + EPSILON)
    filtered = result_all * scale_all
    rounded_orbitals = jnp.concatenate(rounded_parts, axis=3).reshape(point_total, NORB)
    rounded_image = jnp.concatenate(image_parts, axis=3).reshape(point_total, NORB)
    pair_scale = scale_all[:, None] * scale_all[None, :] / point_total
    hamiltonian_block = contract_points(rounded_orbitals, rounded_image) * pair_scale
    margin_block = contract_points(rounded_orbitals, rounded_orbitals) * pair_scale
    return (filtered, hamiltonian_block, margin_block)
```

```python
import jax
import jax.numpy as jnp
from jax import lax
from jax.sharding import PartitionSpec as P

DEGREE = 4


STENCIL = (-205.0 / 72.0, 8.0 / 5.0, -1.0 / 5.0, 8.0 / 315.0, -1.0 / 560.0)
LOWER_EDGE = -2.0
CUT_EDGE = 1.5
UPPER_EDGE = 10.0
EPSILON = 1e-06


def halo_layers(shard, width):
    size = lax.axis_size("grid")
    length = shard.shape[0]
    up = [(i, i + 1) for i in range(size - 1)]
    down = [(j, i) for i, j in up]
    last = lax.slice_in_dim(shard, length - width, length, axis=0).astype(jnp.bfloat16)
    initial = lax.slice_in_dim(shard, 0, width, axis=0).astype(jnp.bfloat16)
    before = lax.ppermute(last, "grid", up).astype(shard.dtype)
    after = lax.ppermute(initial, "grid", down).astype(shard.dtype)
    return jnp.concatenate([before, shard, after], axis=0)


def plane_matrix(rows_y, cols_x):
    flat_count = rows_y * cols_x
    index_all = jnp.arange(flat_count, dtype=jnp.int32)
    row_y = (index_all // cols_x)[:, None]
    row_x = (index_all % cols_x)[:, None]
    col_y = (index_all // cols_x)[None, :]
    col_x = (index_all % cols_x)[None, :]
    delta_y = jnp.mod(row_y - col_y, rows_y)
    delta_x = jnp.mod(row_x - col_x, cols_x)
    same_y = delta_y == 0
    same_x = delta_x == 0
    matrix = jnp.zeros((flat_count, flat_count), jnp.float32)
    for offset in range(1, 5):
        for signed in (offset, -offset):
            hit_y = jnp.logical_and(same_x, delta_y == signed % rows_y)
            hit_x = jnp.logical_and(same_y, delta_x == signed % cols_x)
            matrix = matrix + STENCIL[offset] * (
                hit_y.astype(jnp.float32) + hit_x.astype(jnp.float32)
            )
    return matrix


def apply_hamiltonian(current, potential, plane):
    layers, rows_y, cols_x, width = current.shape
    padded = halo_layers(current, 4)
    laplacian = 3.0 * STENCIL[0] * current
    for offset in range(1, 5):
        laplacian = laplacian + STENCIL[offset] * (
            padded[4 + offset : 4 + offset + layers] + padded[4 - offset : 4 - offset + layers]
        )
    flat = current.reshape(layers, rows_y * cols_x, width)
    in_plane = jnp.einsum(
        "pq,zqo->zpo",
        plane,
        flat,
        precision=lax.Precision.HIGHEST,
        preferred_element_type=jnp.float32,
    )
    laplacian = laplacian + in_plane.reshape(current.shape)
    return -0.5 * laplacian + potential[:, :, :, None] * current


def chebyshev(initial, potential, plane):
    half_width = (UPPER_EDGE - CUT_EDGE) / 2.0
    centre = (UPPER_EDGE + CUT_EDGE) / 2.0
    sigma_now = half_width / (LOWER_EDGE - centre)
    gamma_ratio = 2.0 / sigma_now
    previous = initial
    current = (
        sigma_now / half_width * (apply_hamiltonian(previous, potential, plane) - centre * previous)
    )
    for degree_step in range(DEGREE - 1):
        sigma_next = 1.0 / (gamma_ratio - sigma_now)
        following = (
            2.0
            * sigma_next
            / half_width
            * (apply_hamiltonian(current, potential, plane) - centre * current)
            - sigma_now * sigma_next * previous
        )
        previous, current, sigma_now = (current, following, sigma_next)
    return current


def contract_points(left_side, right_side):
    return lax.dot_general(
        left_side, right_side, (((0,), (0,)), ((), ())), preferred_element_type=jnp.float32
    )


def reduce_scatter_grid(slots):
    size = slots.shape[0]
    bits = size.bit_length() - 1
    me = lax.axis_index("grid")
    rest = slots.shape[1:]
    buf = slots.reshape((2,) * bits + rest)
    for bit in range(bits):
        axis = bits - 1 - bit
        mine = (me >> bit) & 1
        low = lax.index_in_dim(buf, 0, axis=axis, keepdims=False)
        high = lax.index_in_dim(buf, 1, axis=axis, keepdims=False)
        keep = jnp.where(mine == 1, high, low)
        send = jnp.where(mine == 1, low, high)
        pairs = [(i, i ^ (1 << bit)) for i in range(size)]
        buf = keep + lax.ppermute(send, "grid", pairs)
    return buf


def on_device(orbitals, potential):
    own_width = orbitals.shape[3]
    point_count = orbitals.shape[0] * orbitals.shape[1] * orbitals.shape[2]
    grid_size = lax.axis_size("grid")
    point_total = float(point_count * grid_size)
    plane = plane_matrix(orbitals.shape[1], orbitals.shape[2])
    result_block = chebyshev(orbitals, potential, plane)
    own_squares = jnp.sum(result_block * result_block, axis=(0, 1, 2))
    rounded_orbitals = result_block.astype(jnp.bfloat16).reshape(point_count, own_width)
    rounded_image = (
        apply_hamiltonian(result_block, potential, plane)
        .astype(jnp.bfloat16)
        .reshape(point_count, own_width)
    )
    orbitals_all = lax.all_gather(rounded_orbitals, "orb", axis=1, tiled=True)
    total_width = orbitals_all.shape[1]
    rows = total_width // grid_size
    hamiltonian_part = contract_points(orbitals_all, rounded_image)
    margin_part = contract_points(orbitals_all, rounded_orbitals)
    wide = orbitals_all.astype(jnp.float32)
    column_squares = jnp.sum(wide * wide, axis=0)
    body = jnp.concatenate(
        [
            hamiltonian_part.reshape(grid_size, rows, own_width),
            margin_part.reshape(grid_size, rows, own_width),
        ],
        axis=2,
    )
    tail = jnp.concatenate(
        [
            column_squares.reshape(grid_size, rows),
            jnp.broadcast_to(own_squares[None, :], (grid_size, own_width)),
            jnp.zeros((grid_size, own_width - rows), jnp.float32),
        ],
        axis=1,
    )
    slots = jnp.concatenate([body, tail[:, None, :]], axis=1)
    combined = reduce_scatter_grid(slots)
    scale_own = 1.0 / jnp.sqrt(combined[rows, rows : rows + own_width] / point_total + EPSILON)
    column_scale = 1.0 / jnp.sqrt(combined[rows, :rows] / point_total + EPSILON)
    filtered = result_block * scale_own
    pair_scale = scale_own[:, None] * column_scale[None, :] / point_total
    hamiltonian_block = combined[:rows, :own_width].T * pair_scale
    margin_block = combined[:rows, own_width:].T * pair_scale
    return (filtered, hamiltonian_block, margin_block)


def solution(mesh):
    placed = (P("grid", None, None, "orb"), P("grid", None, None))
    return jax.shard_map(
        on_device,
        mesh=mesh,
        in_specs=placed,
        out_specs=(P("grid", None, None, "orb"), P("orb", "grid"), P("orb", "grid")),
        check_vma=False,
    )
```

```python
import jax
import jax.numpy as jnp
from jax import lax
from jax.sharding import PartitionSpec as P

DEGREE = 4


STENCIL = (-205.0 / 72.0, 8.0 / 5.0, -1.0 / 5.0, 8.0 / 315.0, -1.0 / 560.0)
LOWER_EDGE = -2.0
CUT_EDGE = 1.5
UPPER_EDGE = 10.0
EPSILON = 1e-06


def halo_layers(shard, width):
    size = lax.axis_size("grid")
    length = shard.shape[0]
    up = [(i, i + 1) for i in range(size - 1)]
    down = [(j, i) for i, j in up]
    last = lax.slice_in_dim(shard, length - width, length, axis=0).astype(jnp.bfloat16)
    initial = lax.slice_in_dim(shard, 0, width, axis=0).astype(jnp.bfloat16)
    before = lax.ppermute(last, "grid", up).astype(shard.dtype)
    after = lax.ppermute(initial, "grid", down).astype(shard.dtype)
    return jnp.concatenate([before, shard, after], axis=0)


def plane_matrix(rows_y, cols_x):
    flat_count = rows_y * cols_x
    index_all = jnp.arange(flat_count, dtype=jnp.int32)
    row_y = (index_all // cols_x)[:, None]
    row_x = (index_all % cols_x)[:, None]
    col_y = (index_all // cols_x)[None, :]
    col_x = (index_all % cols_x)[None, :]
    delta_y = jnp.mod(row_y - col_y, rows_y)
    delta_x = jnp.mod(row_x - col_x, cols_x)
    same_y = delta_y == 0
    same_x = delta_x == 0
    matrix = jnp.zeros((flat_count, flat_count), jnp.float32)
    for offset in range(1, 5):
        for signed in (offset, -offset):
            hit_y = jnp.logical_and(same_x, delta_y == signed % rows_y)
            hit_x = jnp.logical_and(same_y, delta_x == signed % cols_x)
            matrix = matrix + STENCIL[offset] * (
                hit_y.astype(jnp.float32) + hit_x.astype(jnp.float32)
            )
    return matrix


def apply_hamiltonian(current, potential, plane):
    layers, rows_y, cols_x, width = current.shape
    padded = halo_layers(current, 4)
    laplacian = 3.0 * STENCIL[0] * current
    for offset in range(1, 5):
        laplacian = laplacian + STENCIL[offset] * (
            padded[4 + offset : 4 + offset + layers] + padded[4 - offset : 4 - offset + layers]
        )
    flat = current.reshape(layers, rows_y * cols_x, width)
    in_plane = jnp.einsum(
        "pq,zqo->zpo",
        plane,
        flat,
        precision=lax.Precision.HIGHEST,
        preferred_element_type=jnp.float32,
    )
    laplacian = laplacian + in_plane.reshape(current.shape)
    return -0.5 * laplacian + potential[:, :, :, None] * current


def chebyshev(initial, potential, plane):
    half_width = (UPPER_EDGE - CUT_EDGE) / 2.0
    centre = (UPPER_EDGE + CUT_EDGE) / 2.0
    sigma_now = half_width / (LOWER_EDGE - centre)
    gamma_ratio = 2.0 / sigma_now
    previous = initial
    current = (
        sigma_now / half_width * (apply_hamiltonian(previous, potential, plane) - centre * previous)
    )
    for degree_step in range(DEGREE - 1):
        sigma_next = 1.0 / (gamma_ratio - sigma_now)
        following = (
            2.0
            * sigma_next
            / half_width
            * (apply_hamiltonian(current, potential, plane) - centre * current)
            - sigma_now * sigma_next * previous
        )
        previous, current, sigma_now = (current, following, sigma_next)
    return current


def contract_points(left_side, right_side):
    return lax.dot_general(
        left_side, right_side, (((0,), (0,)), ((), ())), preferred_element_type=jnp.float32
    )


def reduce_scatter_grid(slots):
    received = lax.all_to_all(slots, "grid", 0, 0, tiled=True)
    return jnp.sum(received, axis=0)


def gather_ring(block):
    size = lax.axis_size("orb")
    right = [(i, (i + 1) % size) for i in range(size)]
    left = [(i, (i - 1) % size) for i in range(size)]
    ahead = {0: block}
    from_left, from_right = block, block
    for step in range(1, size // 2 + 1):
        from_left = lax.ppermute(from_left, "orb", right)
        ahead[size - step] = from_left
        if step <= (size - 1) // 2:
            from_right = lax.ppermute(from_right, "orb", left)
            ahead[step] = from_right
    return jnp.concatenate([ahead[k] for k in range(size)], axis=1)


def on_device(orbitals, potential):
    own_width = orbitals.shape[3]
    point_count = orbitals.shape[0] * orbitals.shape[1] * orbitals.shape[2]
    grid_size = lax.axis_size("grid")
    point_total = float(point_count * grid_size)
    plane = plane_matrix(orbitals.shape[1], orbitals.shape[2])
    result_block = chebyshev(orbitals, potential, plane)
    own_squares = jnp.sum(result_block * result_block, axis=(0, 1, 2))
    rounded_orbitals = result_block.astype(jnp.bfloat16).reshape(point_count, own_width)
    rounded_image = (
        apply_hamiltonian(result_block, potential, plane)
        .astype(jnp.bfloat16)
        .reshape(point_count, own_width)
    )
    orbitals_all = gather_ring(rounded_orbitals)
    total_width = orbitals_all.shape[1]
    rows = total_width // grid_size
    hamiltonian_part = contract_points(orbitals_all, rounded_image)
    margin_part = contract_points(orbitals_all, rounded_orbitals)
    wide = orbitals_all.astype(jnp.float32)
    column_squares = jnp.sum(wide * wide, axis=0)
    body = jnp.concatenate(
        [
            hamiltonian_part.reshape(grid_size, rows, own_width),
            margin_part.reshape(grid_size, rows, own_width),
        ],
        axis=2,
    )
    tail = jnp.concatenate(
        [
            column_squares.reshape(grid_size, rows),
            jnp.broadcast_to(own_squares[None, :], (grid_size, own_width)),
            jnp.zeros((grid_size, own_width - rows), jnp.float32),
        ],
        axis=1,
    )
    slots = jnp.concatenate([body, tail[:, None, :]], axis=1)
    slots = jnp.roll(slots, lax.axis_index("orb") * (grid_size * own_width // total_width), axis=0)
    combined = reduce_scatter_grid(slots)
    scale_own = 1.0 / jnp.sqrt(combined[rows, rows : rows + own_width] / point_total + EPSILON)
    column_scale = 1.0 / jnp.sqrt(combined[rows, :rows] / point_total + EPSILON)
    filtered = result_block * scale_own
    pair_scale = scale_own[:, None] * column_scale[None, :] / point_total
    hamiltonian_block = combined[:rows, :own_width].T * pair_scale
    margin_block = combined[:rows, own_width:].T * pair_scale
    return (filtered, hamiltonian_block, margin_block)


def solution(mesh):
    placed = (P("grid", None, None, "orb"), P("grid", None, None))
    return jax.shard_map(
        on_device,
        mesh=mesh,
        in_specs=placed,
        out_specs=(P("grid", None, None, "orb"), P("orb", "grid"), P("orb", "grid")),
        check_vma=False,
    )
```

```python
import jax
import jax.numpy as jnp
from jax import lax
from jax.sharding import PartitionSpec as P

DEGREE = 4


STENCIL = (-205.0 / 72.0, 8.0 / 5.0, -1.0 / 5.0, 8.0 / 315.0, -1.0 / 560.0)
LOWER_EDGE = -2.0
CUT_EDGE = 1.5
UPPER_EDGE = 10.0
EPSILON = 1e-06


def halo_layers(shard, width):
    size = lax.axis_size("grid")
    length = shard.shape[0]
    up = [(i, i + 1) for i in range(size - 1)]
    down = [(j, i) for i, j in up]
    last = lax.slice_in_dim(shard, length - width, length, axis=0).astype(jnp.bfloat16)
    initial = lax.slice_in_dim(shard, 0, width, axis=0).astype(jnp.bfloat16)
    before = lax.ppermute(last, "grid", up).astype(shard.dtype)
    after = lax.ppermute(initial, "grid", down).astype(shard.dtype)
    return jnp.concatenate([before, shard, after], axis=0)


def plane_matrix(rows_y, cols_x):
    flat_count = rows_y * cols_x
    index_all = jnp.arange(flat_count, dtype=jnp.int32)
    row_y = (index_all // cols_x)[:, None]
    row_x = (index_all % cols_x)[:, None]
    col_y = (index_all // cols_x)[None, :]
    col_x = (index_all % cols_x)[None, :]
    delta_y = jnp.mod(row_y - col_y, rows_y)
    delta_x = jnp.mod(row_x - col_x, cols_x)
    same_y = delta_y == 0
    same_x = delta_x == 0
    matrix = jnp.zeros((flat_count, flat_count), jnp.float32)
    for offset in range(1, 5):
        for signed in (offset, -offset):
            hit_y = jnp.logical_and(same_x, delta_y == signed % rows_y)
            hit_x = jnp.logical_and(same_y, delta_x == signed % cols_x)
            matrix = matrix + STENCIL[offset] * (
                hit_y.astype(jnp.float32) + hit_x.astype(jnp.float32)
            )
    return matrix


def apply_hamiltonian(current, potential, plane):
    layers, rows_y, cols_x, width = current.shape
    padded = halo_layers(current, 4)
    laplacian = 3.0 * STENCIL[0] * current
    for offset in range(1, 5):
        laplacian = laplacian + STENCIL[offset] * (
            padded[4 + offset : 4 + offset + layers] + padded[4 - offset : 4 - offset + layers]
        )
    flat = current.reshape(layers, rows_y * cols_x, width)
    in_plane = jnp.einsum(
        "pq,zqo->zpo",
        plane,
        flat,
        precision=lax.Precision.HIGHEST,
        preferred_element_type=jnp.float32,
    )
    laplacian = laplacian + in_plane.reshape(current.shape)
    return -0.5 * laplacian + potential[:, :, :, None] * current


def chebyshev(initial, potential, plane):
    half_width = (UPPER_EDGE - CUT_EDGE) / 2.0
    centre = (UPPER_EDGE + CUT_EDGE) / 2.0
    sigma_now = half_width / (LOWER_EDGE - centre)
    gamma_ratio = 2.0 / sigma_now
    previous = initial
    current = (
        sigma_now / half_width * (apply_hamiltonian(previous, potential, plane) - centre * previous)
    )
    for degree_step in range(DEGREE - 1):
        sigma_next = 1.0 / (gamma_ratio - sigma_now)
        following = (
            2.0
            * sigma_next
            / half_width
            * (apply_hamiltonian(current, potential, plane) - centre * current)
            - sigma_now * sigma_next * previous
        )
        previous, current, sigma_now = (current, following, sigma_next)
    return current


def contract_points(left_side, right_side):
    return lax.dot_general(
        left_side, right_side, (((0,), (0,)), ((), ())), preferred_element_type=jnp.float32
    )


def stage_sizes(size):
    sizes = [2]
    middle = min(8, size // 2)
    sizes.append(middle)
    if size // (2 * middle) > 1:
        sizes.append(size // (2 * middle))
    return sizes


def reduce_scatter_grid(slots):
    size = slots.shape[0]
    payload = slots.shape[1:]
    me = lax.axis_index("grid")
    buf = slots
    stride = 1
    for count in stage_sizes(size):
        buf = buf.reshape((-1, count) + payload)
        digit = (me // stride) % count
        rel = jnp.roll(buf, -digit, axis=1)
        total = rel[:, 0]
        for shift in range(1, count):
            pairs = []
            for i in range(size):
                d = (i // stride) % count
                pairs.append((i, i + ((d + shift) % count - d) * stride))
            total = total + lax.ppermute(rel[:, shift], "grid", pairs)
        buf = total
        stride *= count
    return buf.reshape(payload)


def gather_ring(block):
    size = lax.axis_size("orb")
    right = [(i, (i + 1) % size) for i in range(size)]
    left = [(i, (i - 1) % size) for i in range(size)]
    ahead = {0: block}
    from_left, from_right = block, block
    for step in range(1, size // 2 + 1):
        from_left = lax.ppermute(from_left, "orb", right)
        ahead[size - step] = from_left
        if step <= (size - 1) // 2:
            from_right = lax.ppermute(from_right, "orb", left)
            ahead[step] = from_right
    return jnp.concatenate([ahead[k] for k in range(size)], axis=1)


def on_device(orbitals, potential):
    own_width = orbitals.shape[3]
    point_count = orbitals.shape[0] * orbitals.shape[1] * orbitals.shape[2]
    grid_size = lax.axis_size("grid")
    point_total = float(point_count * grid_size)
    plane = plane_matrix(orbitals.shape[1], orbitals.shape[2])
    result_block = chebyshev(orbitals, potential, plane)
    own_squares = jnp.sum(result_block * result_block, axis=(0, 1, 2))
    rounded_orbitals = result_block.astype(jnp.bfloat16).reshape(point_count, own_width)
    rounded_image = (
        apply_hamiltonian(result_block, potential, plane)
        .astype(jnp.bfloat16)
        .reshape(point_count, own_width)
    )
    orbitals_all = gather_ring(rounded_orbitals)
    total_width = orbitals_all.shape[1]
    rows = total_width // grid_size
    hamiltonian_part = contract_points(orbitals_all, rounded_image)
    margin_part = contract_points(orbitals_all, rounded_orbitals)
    wide = orbitals_all.astype(jnp.float32)
    column_squares = jnp.sum(wide * wide, axis=0)
    body = jnp.concatenate(
        [
            hamiltonian_part.reshape(grid_size, rows, own_width),
            margin_part.reshape(grid_size, rows, own_width),
        ],
        axis=2,
    )
    tail = jnp.concatenate(
        [
            column_squares.reshape(grid_size, rows),
            jnp.broadcast_to(own_squares[None, :], (grid_size, own_width)),
            jnp.zeros((grid_size, own_width - rows), jnp.float32),
        ],
        axis=1,
    )
    slots = jnp.concatenate([body, tail[:, None, :]], axis=1)
    slots = jnp.roll(slots, lax.axis_index("orb") * (grid_size * own_width // total_width), axis=0)
    combined = reduce_scatter_grid(slots)
    scale_own = 1.0 / jnp.sqrt(combined[rows, rows : rows + own_width] / point_total + EPSILON)
    column_scale = 1.0 / jnp.sqrt(combined[rows, :rows] / point_total + EPSILON)
    filtered = result_block * scale_own
    pair_scale = scale_own[:, None] * column_scale[None, :] / point_total
    hamiltonian_block = combined[:rows, :own_width].T * pair_scale
    margin_block = combined[:rows, own_width:].T * pair_scale
    return (filtered, hamiltonian_block, margin_block)


def solution(mesh):
    placed = (P("grid", None, None, "orb"), P("grid", None, None))
    return jax.shard_map(
        on_device,
        mesh=mesh,
        in_specs=placed,
        out_specs=(P("grid", None, None, "orb"), P("orb", "grid"), P("orb", "grid")),
        check_vma=False,
    )
```

```python
import jax
import jax.numpy as jnp
from jax import lax
from jax.sharding import PartitionSpec as P

DEGREE = 4


STENCIL = (-205.0 / 72.0, 8.0 / 5.0, -1.0 / 5.0, 8.0 / 315.0, -1.0 / 560.0)
LOWER_EDGE = -2.0
CUT_EDGE = 1.5
UPPER_EDGE = 10.0
EPSILON = 1e-06


def halo_layers(shard, width):
    size = lax.axis_size("grid")
    length = shard.shape[0]
    up = [(i, i + 1) for i in range(size - 1)]
    down = [(j, i) for i, j in up]
    last = lax.slice_in_dim(shard, length - width, length, axis=0).astype(jnp.bfloat16)
    initial = lax.slice_in_dim(shard, 0, width, axis=0).astype(jnp.bfloat16)
    before = lax.ppermute(last, "grid", up).astype(shard.dtype)
    after = lax.ppermute(initial, "grid", down).astype(shard.dtype)
    return jnp.concatenate([before, shard, after], axis=0)


def plane_matrix(rows_y, cols_x):
    flat_count = rows_y * cols_x
    index_all = jnp.arange(flat_count, dtype=jnp.int32)
    row_y = (index_all // cols_x)[:, None]
    row_x = (index_all % cols_x)[:, None]
    col_y = (index_all // cols_x)[None, :]
    col_x = (index_all % cols_x)[None, :]
    delta_y = jnp.mod(row_y - col_y, rows_y)
    delta_x = jnp.mod(row_x - col_x, cols_x)
    same_y = delta_y == 0
    same_x = delta_x == 0
    matrix = jnp.zeros((flat_count, flat_count), jnp.float32)
    for offset in range(1, 5):
        for signed in (offset, -offset):
            hit_y = jnp.logical_and(same_x, delta_y == signed % rows_y)
            hit_x = jnp.logical_and(same_y, delta_x == signed % cols_x)
            matrix = matrix + STENCIL[offset] * (
                hit_y.astype(jnp.float32) + hit_x.astype(jnp.float32)
            )
    return matrix


def apply_hamiltonian(current, potential, plane):
    layers, rows_y, cols_x, width = current.shape
    padded = halo_layers(current, 4)
    laplacian = 3.0 * STENCIL[0] * current
    for offset in range(1, 5):
        laplacian = laplacian + STENCIL[offset] * (
            padded[4 + offset : 4 + offset + layers] + padded[4 - offset : 4 - offset + layers]
        )
    flat = current.reshape(layers, rows_y * cols_x, width)
    in_plane = jnp.einsum(
        "pq,zqo->zpo",
        plane,
        flat,
        precision=lax.Precision.HIGHEST,
        preferred_element_type=jnp.float32,
    )
    laplacian = laplacian + in_plane.reshape(current.shape)
    return -0.5 * laplacian + potential[:, :, :, None] * current


def chebyshev(initial, potential, plane):
    half_width = (UPPER_EDGE - CUT_EDGE) / 2.0
    centre = (UPPER_EDGE + CUT_EDGE) / 2.0
    sigma_now = half_width / (LOWER_EDGE - centre)
    gamma_ratio = 2.0 / sigma_now
    previous = initial
    current = (
        sigma_now / half_width * (apply_hamiltonian(previous, potential, plane) - centre * previous)
    )
    for degree_step in range(DEGREE - 1):
        sigma_next = 1.0 / (gamma_ratio - sigma_now)
        following = (
            2.0
            * sigma_next
            / half_width
            * (apply_hamiltonian(current, potential, plane) - centre * current)
            - sigma_now * sigma_next * previous
        )
        previous, current, sigma_now = (current, following, sigma_next)
    return current


def contract_points(left_side, right_side):
    return lax.dot_general(
        left_side, right_side, (((0,), (0,)), ((), ())), preferred_element_type=jnp.float32
    )


def halving_order(bits):
    order = [0, 1, 4, 2, 5, 3]
    if bits != 6:
        order = list(range(bits))
    return order


def reduce_scatter_grid(slots):
    size = slots.shape[0]
    bits = size.bit_length() - 1
    me = lax.axis_index("grid")
    rest = slots.shape[1:]
    buf = slots.reshape((2,) * bits + rest)
    remaining = list(range(bits - 1, -1, -1))
    for bit in halving_order(bits):
        axis = remaining.index(bit)
        remaining.remove(bit)
        mine = (me >> bit) & 1
        low = lax.index_in_dim(buf, 0, axis=axis, keepdims=False)
        high = lax.index_in_dim(buf, 1, axis=axis, keepdims=False)
        keep = jnp.where(mine == 1, high, low)
        send = jnp.where(mine == 1, low, high)
        pairs = [(i, i ^ (1 << bit)) for i in range(size)]
        buf = keep + lax.ppermute(send, "grid", pairs)
    return buf


def gather_ring(block):
    size = lax.axis_size("orb")
    right = [(i, (i + 1) % size) for i in range(size)]
    left = [(i, (i - 1) % size) for i in range(size)]
    ahead = {0: block}
    from_left, from_right = block, block
    for step in range(1, size // 2 + 1):
        from_left = lax.ppermute(from_left, "orb", right)
        ahead[size - step] = from_left
        if step <= (size - 1) // 2:
            from_right = lax.ppermute(from_right, "orb", left)
            ahead[step] = from_right
    return jnp.concatenate([ahead[k] for k in range(size)], axis=1)


def on_device(orbitals, potential):
    own_width = orbitals.shape[3]
    point_count = orbitals.shape[0] * orbitals.shape[1] * orbitals.shape[2]
    grid_size = lax.axis_size("grid")
    point_total = float(point_count * grid_size)
    plane = plane_matrix(orbitals.shape[1], orbitals.shape[2])
    result_block = chebyshev(orbitals, potential, plane)
    own_squares = jnp.sum(result_block * result_block, axis=(0, 1, 2))
    rounded_orbitals = result_block.astype(jnp.bfloat16).reshape(point_count, own_width)
    rounded_image = (
        apply_hamiltonian(result_block, potential, plane)
        .astype(jnp.bfloat16)
        .reshape(point_count, own_width)
    )
    orbitals_all = gather_ring(rounded_orbitals)
    total_width = orbitals_all.shape[1]
    rows = total_width // grid_size
    hamiltonian_part = contract_points(orbitals_all, rounded_image)
    margin_part = contract_points(orbitals_all, rounded_orbitals)
    wide = orbitals_all.astype(jnp.float32)
    column_squares = jnp.sum(wide * wide, axis=0)
    body = jnp.concatenate(
        [
            hamiltonian_part.reshape(grid_size, rows, own_width),
            margin_part.reshape(grid_size, rows, own_width),
        ],
        axis=2,
    )
    tail = jnp.concatenate(
        [
            column_squares.reshape(grid_size, rows),
            jnp.broadcast_to(own_squares[None, :], (grid_size, own_width)),
            jnp.zeros((grid_size, own_width - rows), jnp.float32),
        ],
        axis=1,
    )
    slots = jnp.concatenate([body, tail[:, None, :]], axis=1)
    slots = jnp.roll(slots, lax.axis_index("orb") * (grid_size * own_width // total_width), axis=0)
    combined = reduce_scatter_grid(slots)
    scale_own = 1.0 / jnp.sqrt(combined[rows, rows : rows + own_width] / point_total + EPSILON)
    column_scale = 1.0 / jnp.sqrt(combined[rows, :rows] / point_total + EPSILON)
    filtered = result_block * scale_own
    pair_scale = scale_own[:, None] * column_scale[None, :] / point_total
    hamiltonian_block = combined[:rows, :own_width].T * pair_scale
    margin_block = combined[:rows, own_width:].T * pair_scale
    return (filtered, hamiltonian_block, margin_block)


def solution(mesh):
    placed = (P("grid", None, None, "orb"), P("grid", None, None))
    return jax.shard_map(
        on_device,
        mesh=mesh,
        in_specs=placed,
        out_specs=(P("grid", None, None, "orb"), P("orb", "grid"), P("orb", "grid")),
        check_vma=False,
    )
```

```python
import jax
import jax.numpy as jnp
from jax import lax
from jax.sharding import Mesh, PartitionSpec as P

DEGREE = 4
GRID = ("chip", "core")


STENCIL = (-205.0 / 72.0, 8.0 / 5.0, -1.0 / 5.0, 8.0 / 315.0, -1.0 / 560.0)
LOWER_EDGE = -2.0
CUT_EDGE = 1.5
UPPER_EDGE = 10.0
EPSILON = 1e-06


def halo_layers(shard, width):
    size = lax.axis_size(GRID)
    length = shard.shape[0]
    up = [(i, i + 1) for i in range(size - 1)]
    down = [(j, i) for i, j in up]
    last = lax.slice_in_dim(shard, length - width, length, axis=0).astype(jnp.bfloat16)
    initial = lax.slice_in_dim(shard, 0, width, axis=0).astype(jnp.bfloat16)
    before = lax.ppermute(last, GRID, up).astype(shard.dtype)
    after = lax.ppermute(initial, GRID, down).astype(shard.dtype)
    return jnp.concatenate([before, shard, after], axis=0)


def plane_matrix(rows_y, cols_x):
    flat_count = rows_y * cols_x
    index_all = jnp.arange(flat_count, dtype=jnp.int32)
    row_y = (index_all // cols_x)[:, None]
    row_x = (index_all % cols_x)[:, None]
    col_y = (index_all // cols_x)[None, :]
    col_x = (index_all % cols_x)[None, :]
    delta_y = jnp.mod(row_y - col_y, rows_y)
    delta_x = jnp.mod(row_x - col_x, cols_x)
    same_y = delta_y == 0
    same_x = delta_x == 0
    matrix = jnp.zeros((flat_count, flat_count), jnp.float32)
    for offset in range(1, 5):
        for signed in (offset, -offset):
            hit_y = jnp.logical_and(same_x, delta_y == signed % rows_y)
            hit_x = jnp.logical_and(same_y, delta_x == signed % cols_x)
            matrix = matrix + STENCIL[offset] * (
                hit_y.astype(jnp.float32) + hit_x.astype(jnp.float32)
            )
    return matrix


def apply_hamiltonian(current, potential, plane):
    layers, rows_y, cols_x, width = current.shape
    padded = halo_layers(current, 4)
    laplacian = 3.0 * STENCIL[0] * current
    for offset in range(1, 5):
        laplacian = laplacian + STENCIL[offset] * (
            padded[4 + offset : 4 + offset + layers] + padded[4 - offset : 4 - offset + layers]
        )
    flat = current.reshape(layers, rows_y * cols_x, width)
    in_plane = jnp.einsum(
        "pq,zqo->zpo",
        plane,
        flat,
        precision=lax.Precision.HIGHEST,
        preferred_element_type=jnp.float32,
    )
    laplacian = laplacian + in_plane.reshape(current.shape)
    return -0.5 * laplacian + potential[:, :, :, None] * current


def chebyshev(initial, potential, plane):
    half_width = (UPPER_EDGE - CUT_EDGE) / 2.0
    centre = (UPPER_EDGE + CUT_EDGE) / 2.0
    sigma_now = half_width / (LOWER_EDGE - centre)
    gamma_ratio = 2.0 / sigma_now
    previous = initial
    current = (
        sigma_now / half_width * (apply_hamiltonian(previous, potential, plane) - centre * previous)
    )
    for degree_step in range(DEGREE - 1):
        sigma_next = 1.0 / (gamma_ratio - sigma_now)
        following = (
            2.0
            * sigma_next
            / half_width
            * (apply_hamiltonian(current, potential, plane) - centre * current)
            - sigma_now * sigma_next * previous
        )
        previous, current, sigma_now = (current, following, sigma_next)
    return current


def contract_points(left_side, right_side):
    return lax.dot_general(
        left_side, right_side, (((0,), (0,)), ((), ())), preferred_element_type=jnp.float32
    )


def reduce_scatter_grid(slots):
    pairs = lax.axis_size("core")
    mine = lax.axis_index("core")
    split = slots.reshape((slots.shape[0] // pairs, pairs) + slots.shape[1:])
    low, high = split[:, 0], split[:, 1]
    keep = jnp.where(mine == 1, high, low)
    send = jnp.where(mine == 1, low, high)
    chip_part = keep + lax.ppermute(send, "core", [(0, 1), (1, 0)])
    received = lax.all_to_all(chip_part, "chip", 0, 0, tiled=True)
    return jnp.sum(received, axis=0)


def gather_ring(block):
    size = lax.axis_size("orb")
    right = [(i, (i + 1) % size) for i in range(size)]
    left = [(i, (i - 1) % size) for i in range(size)]
    ahead = {0: block}
    from_left, from_right = block, block
    for step in range(1, size // 2 + 1):
        from_left = lax.ppermute(from_left, "orb", right)
        ahead[size - step] = from_left
        if step <= (size - 1) // 2:
            from_right = lax.ppermute(from_right, "orb", left)
            ahead[step] = from_right
    return jnp.concatenate([ahead[k] for k in range(size)], axis=1)


def on_device(orbitals, potential):
    own_width = orbitals.shape[3]
    point_count = orbitals.shape[0] * orbitals.shape[1] * orbitals.shape[2]
    grid_size = lax.axis_size(GRID)
    point_total = float(point_count * grid_size)
    plane = plane_matrix(orbitals.shape[1], orbitals.shape[2])
    result_block = chebyshev(orbitals, potential, plane)
    own_squares = jnp.sum(result_block * result_block, axis=(0, 1, 2))
    rounded_orbitals = result_block.astype(jnp.bfloat16).reshape(point_count, own_width)
    rounded_image = (
        apply_hamiltonian(result_block, potential, plane)
        .astype(jnp.bfloat16)
        .reshape(point_count, own_width)
    )
    orbitals_all = gather_ring(rounded_orbitals)
    total_width = orbitals_all.shape[1]
    rows = total_width // grid_size
    hamiltonian_part = contract_points(orbitals_all, rounded_image)
    margin_part = contract_points(orbitals_all, rounded_orbitals)
    wide = orbitals_all.astype(jnp.float32)
    column_squares = jnp.sum(wide * wide, axis=0)
    body = jnp.concatenate(
        [
            hamiltonian_part.reshape(grid_size, rows, own_width),
            margin_part.reshape(grid_size, rows, own_width),
        ],
        axis=2,
    )
    tail = jnp.concatenate(
        [
            column_squares.reshape(grid_size, rows),
            jnp.broadcast_to(own_squares[None, :], (grid_size, own_width)),
            jnp.zeros((grid_size, own_width - rows), jnp.float32),
        ],
        axis=1,
    )
    slots = jnp.concatenate([body, tail[:, None, :]], axis=1)
    slots = jnp.roll(slots, lax.axis_index("orb") * (grid_size * own_width // total_width), axis=0)
    combined = reduce_scatter_grid(slots)
    scale_own = 1.0 / jnp.sqrt(combined[rows, rows : rows + own_width] / point_total + EPSILON)
    column_scale = 1.0 / jnp.sqrt(combined[rows, :rows] / point_total + EPSILON)
    filtered = result_block * scale_own
    pair_scale = scale_own[:, None] * column_scale[None, :] / point_total
    hamiltonian_block = combined[:rows, :own_width].T * pair_scale
    margin_block = combined[:rows, own_width:].T * pair_scale
    return (filtered, hamiltonian_block, margin_block)


def solution(mesh):
    grid_size, orb_size = mesh.devices.shape
    split_mesh = Mesh(mesh.devices.reshape(grid_size // 2, 2, orb_size), ("chip", "core", "orb"))
    placed = (P(GRID, None, None, "orb"), P(GRID, None, None))
    return jax.shard_map(
        on_device,
        mesh=split_mesh,
        in_specs=placed,
        out_specs=(P(GRID, None, None, "orb"), P("orb", GRID), P("orb", GRID)),
        check_vma=False,
    )
```

```python
import jax
import jax.numpy as jnp
from jax import lax
from jax.sharding import Mesh, PartitionSpec as P

DEGREE = 4
GRID = ("x", "z", "core")


STENCIL = (-205.0 / 72.0, 8.0 / 5.0, -1.0 / 5.0, 8.0 / 315.0, -1.0 / 560.0)
LOWER_EDGE = -2.0
CUT_EDGE = 1.5
UPPER_EDGE = 10.0
EPSILON = 1e-06


def halo_layers(shard, width):
    size = lax.axis_size(GRID)
    length = shard.shape[0]
    up = [(i, i + 1) for i in range(size - 1)]
    down = [(j, i) for i, j in up]
    last = lax.slice_in_dim(shard, length - width, length, axis=0).astype(jnp.bfloat16)
    initial = lax.slice_in_dim(shard, 0, width, axis=0).astype(jnp.bfloat16)
    before = lax.ppermute(last, GRID, up).astype(shard.dtype)
    after = lax.ppermute(initial, GRID, down).astype(shard.dtype)
    return jnp.concatenate([before, shard, after], axis=0)


def plane_matrix(rows_y, cols_x):
    flat_count = rows_y * cols_x
    index_all = jnp.arange(flat_count, dtype=jnp.int32)
    row_y = (index_all // cols_x)[:, None]
    row_x = (index_all % cols_x)[:, None]
    col_y = (index_all // cols_x)[None, :]
    col_x = (index_all % cols_x)[None, :]
    delta_y = jnp.mod(row_y - col_y, rows_y)
    delta_x = jnp.mod(row_x - col_x, cols_x)
    same_y = delta_y == 0
    same_x = delta_x == 0
    matrix = jnp.zeros((flat_count, flat_count), jnp.float32)
    for offset in range(1, 5):
        for signed in (offset, -offset):
            hit_y = jnp.logical_and(same_x, delta_y == signed % rows_y)
            hit_x = jnp.logical_and(same_y, delta_x == signed % cols_x)
            matrix = matrix + STENCIL[offset] * (
                hit_y.astype(jnp.float32) + hit_x.astype(jnp.float32)
            )
    return matrix


def apply_hamiltonian(current, potential, plane):
    layers, rows_y, cols_x, width = current.shape
    padded = halo_layers(current, 4)
    laplacian = 3.0 * STENCIL[0] * current
    for offset in range(1, 5):
        laplacian = laplacian + STENCIL[offset] * (
            padded[4 + offset : 4 + offset + layers] + padded[4 - offset : 4 - offset + layers]
        )
    flat = current.reshape(layers, rows_y * cols_x, width)
    in_plane = jnp.einsum(
        "pq,zqo->zpo",
        plane,
        flat,
        precision=lax.Precision.HIGHEST,
        preferred_element_type=jnp.float32,
    )
    laplacian = laplacian + in_plane.reshape(current.shape)
    return -0.5 * laplacian + potential[:, :, :, None] * current


def chebyshev(initial, potential, plane):
    half_width = (UPPER_EDGE - CUT_EDGE) / 2.0
    centre = (UPPER_EDGE + CUT_EDGE) / 2.0
    sigma_now = half_width / (LOWER_EDGE - centre)
    gamma_ratio = 2.0 / sigma_now
    previous = initial
    current = (
        sigma_now / half_width * (apply_hamiltonian(previous, potential, plane) - centre * previous)
    )
    for degree_step in range(DEGREE - 1):
        sigma_next = 1.0 / (gamma_ratio - sigma_now)
        following = (
            2.0
            * sigma_next
            / half_width
            * (apply_hamiltonian(current, potential, plane) - centre * current)
            - sigma_now * sigma_next * previous
        )
        previous, current, sigma_now = (current, following, sigma_next)
    return current


def contract_points(left_side, right_side):
    return lax.dot_general(
        left_side, right_side, (((0,), (0,)), ((), ())), preferred_element_type=jnp.float32
    )


def reduce_scatter_grid(slots):
    pairs = lax.axis_size("core")
    mine = lax.axis_index("core")
    split = slots.reshape((slots.shape[0] // pairs, pairs) + slots.shape[1:])
    low, high = split[:, 0], split[:, 1]
    keep = jnp.where(mine == 1, high, low)
    send = jnp.where(mine == 1, low, high)
    chip_part = keep + lax.ppermute(send, "core", [(0, 1), (1, 0)])
    chip_part = chip_part.reshape((lax.axis_size("x"), lax.axis_size("z")) + slots.shape[1:])
    row_part = jnp.sum(lax.all_to_all(chip_part, "x", 0, 0, tiled=True), axis=0)
    return jnp.sum(lax.all_to_all(row_part, "z", 0, 0, tiled=True), axis=0)


def gather_ring(block):
    size = lax.axis_size("orb")
    right = [(i, (i + 1) % size) for i in range(size)]
    left = [(i, (i - 1) % size) for i in range(size)]
    ahead = {0: block}
    from_left, from_right = block, block
    for step in range(1, size // 2 + 1):
        from_left = lax.ppermute(from_left, "orb", right)
        ahead[size - step] = from_left
        if step <= (size - 1) // 2:
            from_right = lax.ppermute(from_right, "orb", left)
            ahead[step] = from_right
    return [ahead[k] for k in range(size)]


def on_device(orbitals, potential):
    own_width = orbitals.shape[3]
    point_count = orbitals.shape[0] * orbitals.shape[1] * orbitals.shape[2]
    grid_size = lax.axis_size(GRID)
    point_total = float(point_count * grid_size)
    plane = plane_matrix(orbitals.shape[1], orbitals.shape[2])
    result_block = chebyshev(orbitals, potential, plane)
    own_squares = jnp.sum(result_block * result_block, axis=(0, 1, 2))
    rounded_orbitals = result_block.astype(jnp.bfloat16).reshape(point_count, own_width)
    rounded_image = (
        apply_hamiltonian(result_block, potential, plane)
        .astype(jnp.bfloat16)
        .reshape(point_count, own_width)
    )
    blocks = gather_ring(rounded_orbitals)
    total_width = own_width * len(blocks)
    rows = total_width // grid_size
    hamiltonian_part = jnp.concatenate(
        [contract_points(block, rounded_image) for block in blocks], axis=0
    )
    margin_part = jnp.concatenate(
        [contract_points(block, rounded_orbitals) for block in blocks], axis=0
    )
    column_squares = jnp.concatenate(
        [jnp.sum(jnp.square(block.astype(jnp.float32)), axis=0) for block in blocks], axis=0
    )
    body = jnp.concatenate(
        [
            hamiltonian_part.reshape(grid_size, rows, own_width),
            margin_part.reshape(grid_size, rows, own_width),
        ],
        axis=2,
    )
    tail = jnp.concatenate(
        [
            column_squares.reshape(grid_size, rows),
            jnp.broadcast_to(own_squares[None, :], (grid_size, own_width)),
            jnp.zeros((grid_size, own_width - rows), jnp.float32),
        ],
        axis=1,
    )
    slots = jnp.concatenate([body, tail[:, None, :]], axis=1)
    slots = jnp.roll(slots, lax.axis_index("orb") * (grid_size * own_width // total_width), axis=0)
    combined = reduce_scatter_grid(slots)
    scale_own = 1.0 / jnp.sqrt(combined[rows, rows : rows + own_width] / point_total + EPSILON)
    column_scale = 1.0 / jnp.sqrt(combined[rows, :rows] / point_total + EPSILON)
    filtered = result_block * scale_own
    pair_scale = scale_own[:, None] * column_scale[None, :] / point_total
    hamiltonian_block = combined[:rows, :own_width].T * pair_scale
    margin_block = combined[:rows, own_width:].T * pair_scale
    return (filtered, hamiltonian_block, margin_block)


def solution(mesh):
    grid_size, orb_size = mesh.devices.shape
    z_size = min(8, grid_size // 2)
    split_mesh = Mesh(
        mesh.devices.reshape(grid_size // (2 * z_size), z_size, 2, orb_size), ("x", "z", "core", "orb")
    )
    placed = (P(GRID, None, None, "orb"), P(GRID, None, None))
    return jax.shard_map(
        on_device,
        mesh=split_mesh,
        in_specs=placed,
        out_specs=(P(GRID, None, None, "orb"), P("orb", GRID), P("orb", GRID)),
        check_vma=False,
    )
```

```python
import jax
import jax.numpy as jnp
from jax import lax
from jax.sharding import Mesh, PartitionSpec as P

DEGREE = 4
GRID = ("x", "z", "core")


STENCIL = (-205.0 / 72.0, 8.0 / 5.0, -1.0 / 5.0, 8.0 / 315.0, -1.0 / 560.0)
LOWER_EDGE = -2.0
CUT_EDGE = 1.5
UPPER_EDGE = 10.0
EPSILON = 1e-06


def halo_layers(shard, width):
    size = lax.axis_size(GRID)
    length = shard.shape[0]
    up = [(i, i + 1) for i in range(size - 1)]
    down = [(j, i) for i, j in up]
    last = lax.slice_in_dim(shard, length - width, length, axis=0).astype(jnp.bfloat16)
    initial = lax.slice_in_dim(shard, 0, width, axis=0).astype(jnp.bfloat16)
    before = lax.ppermute(last, GRID, up).astype(shard.dtype)
    after = lax.ppermute(initial, GRID, down).astype(shard.dtype)
    return jnp.concatenate([before, shard, after], axis=0)


def plane_matrix(rows_y, cols_x):
    flat_count = rows_y * cols_x
    index_all = jnp.arange(flat_count, dtype=jnp.int32)
    row_y = (index_all // cols_x)[:, None]
    row_x = (index_all % cols_x)[:, None]
    col_y = (index_all // cols_x)[None, :]
    col_x = (index_all % cols_x)[None, :]
    delta_y = jnp.mod(row_y - col_y, rows_y)
    delta_x = jnp.mod(row_x - col_x, cols_x)
    same_y = delta_y == 0
    same_x = delta_x == 0
    matrix = jnp.zeros((flat_count, flat_count), jnp.float32)
    for offset in range(1, 5):
        for signed in (offset, -offset):
            hit_y = jnp.logical_and(same_x, delta_y == signed % rows_y)
            hit_x = jnp.logical_and(same_y, delta_x == signed % cols_x)
            matrix = matrix + STENCIL[offset] * (
                hit_y.astype(jnp.float32) + hit_x.astype(jnp.float32)
            )
    return matrix


def apply_hamiltonian(current, potential, plane):
    layers, rows_y, cols_x, width = current.shape
    padded = halo_layers(current, 4)
    laplacian = 3.0 * STENCIL[0] * current
    for offset in range(1, 5):
        laplacian = laplacian + STENCIL[offset] * (
            padded[4 + offset : 4 + offset + layers] + padded[4 - offset : 4 - offset + layers]
        )
    flat = current.reshape(layers, rows_y * cols_x, width)
    in_plane = jnp.einsum(
        "pq,zqo->zpo",
        plane,
        flat,
        precision=lax.Precision.HIGH,
        preferred_element_type=jnp.float32,
    )
    laplacian = laplacian + in_plane.reshape(current.shape)
    return -0.5 * laplacian + potential[:, :, :, None] * current


def chebyshev(initial, potential, plane):
    half_width = (UPPER_EDGE - CUT_EDGE) / 2.0
    centre = (UPPER_EDGE + CUT_EDGE) / 2.0
    sigma_now = half_width / (LOWER_EDGE - centre)
    gamma_ratio = 2.0 / sigma_now
    previous = initial
    current = (
        sigma_now / half_width * (apply_hamiltonian(previous, potential, plane) - centre * previous)
    )
    for degree_step in range(DEGREE - 1):
        sigma_next = 1.0 / (gamma_ratio - sigma_now)
        following = (
            2.0
            * sigma_next
            / half_width
            * (apply_hamiltonian(current, potential, plane) - centre * current)
            - sigma_now * sigma_next * previous
        )
        previous, current, sigma_now = (current, following, sigma_next)
    return current


def contract_points(left_side, right_side):
    return lax.dot_general(
        left_side, right_side, (((0,), (0,)), ((), ())), preferred_element_type=jnp.float32
    )


def reduce_scatter_grid(slots):
    pairs = lax.axis_size("core")
    mine = lax.axis_index("core")
    split = slots.reshape((slots.shape[0] // pairs, pairs) + slots.shape[1:])
    low, high = split[:, 0], split[:, 1]
    keep = jnp.where(mine == 1, high, low)
    send = jnp.where(mine == 1, low, high)
    chip_part = keep + lax.ppermute(send, "core", [(0, 1), (1, 0)])
    received = lax.all_to_all(chip_part, ("x", "z"), 0, 0, tiled=True)
    return jnp.sum(received, axis=0)


def shifted(value, shift):
    size = lax.axis_size("orb")
    return lax.ppermute(value, "orb", [(i, (i + shift) % size) for i in range(size)])


def gather_blocks(block):
    if lax.axis_size("orb") != 8:
        return gather_ring(block)
    ahead = {0: block}
    for step in (1, 2):
        ahead[-step] = shifted(block, step)
        ahead[step] = shifted(block, -step)
    half = block.shape[0] // 2
    ahead[3] = shifted(ahead[2], -1)
    ahead[-3] = shifted(ahead[-2], 1)
    ahead[4] = jnp.concatenate(
        [shifted(ahead[2][:half], -2), shifted(ahead[-2][half:], 2)], axis=0
    )
    return [ahead[k] if k <= 4 else ahead[k - 8] for k in range(8)]


def gather_ring(block):
    size = lax.axis_size("orb")
    right = [(i, (i + 1) % size) for i in range(size)]
    left = [(i, (i - 1) % size) for i in range(size)]
    ahead = {0: block}
    from_left, from_right = block, block
    for step in range(1, size // 2 + 1):
        from_left = lax.ppermute(from_left, "orb", right)
        ahead[size - step] = from_left
        if step <= (size - 1) // 2:
            from_right = lax.ppermute(from_right, "orb", left)
            ahead[step] = from_right
    return [ahead[k] for k in range(size)]


def on_device(orbitals, potential):
    own_width = orbitals.shape[3]
    point_count = orbitals.shape[0] * orbitals.shape[1] * orbitals.shape[2]
    grid_size = lax.axis_size(GRID)
    point_total = float(point_count * grid_size)
    plane = plane_matrix(orbitals.shape[1], orbitals.shape[2])
    result_block = chebyshev(orbitals, potential, plane)
    own_squares = jnp.sum(result_block * result_block, axis=(0, 1, 2))
    rounded_orbitals = result_block.astype(jnp.bfloat16).reshape(point_count, own_width)
    rounded_image = (
        apply_hamiltonian(result_block, potential, plane)
        .astype(jnp.bfloat16)
        .reshape(point_count, own_width)
    )
    blocks = gather_blocks(rounded_orbitals)
    total_width = own_width * len(blocks)
    rows = total_width // grid_size
    hamiltonian_part = jnp.concatenate(
        [contract_points(block, rounded_image) for block in blocks], axis=0
    )
    margin_part = jnp.concatenate(
        [contract_points(block, rounded_orbitals) for block in blocks], axis=0
    )
    column_squares = jnp.concatenate(
        [jnp.sum(jnp.square(block.astype(jnp.float32)), axis=0) for block in blocks], axis=0
    )
    body = jnp.concatenate(
        [
            hamiltonian_part.reshape(grid_size, rows, own_width),
            margin_part.reshape(grid_size, rows, own_width),
        ],
        axis=2,
    )
    tail = jnp.concatenate(
        [
            column_squares.reshape(grid_size, rows),
            jnp.broadcast_to(own_squares[None, :], (grid_size, own_width)),
            jnp.zeros((grid_size, own_width - rows), jnp.float32),
        ],
        axis=1,
    )
    slots = jnp.concatenate([body, tail[:, None, :]], axis=1)
    slots = jnp.roll(slots, lax.axis_index("orb") * (grid_size * own_width // total_width), axis=0)
    combined = reduce_scatter_grid(slots)
    scale_own = 1.0 / jnp.sqrt(combined[rows, rows : rows + own_width] / point_total + EPSILON)
    column_scale = 1.0 / jnp.sqrt(combined[rows, :rows] / point_total + EPSILON)
    filtered = result_block * scale_own
    pair_scale = scale_own[:, None] * column_scale[None, :] / point_total
    hamiltonian_block = combined[:rows, :own_width].T * pair_scale
    margin_block = combined[:rows, own_width:].T * pair_scale
    return (filtered, hamiltonian_block, margin_block)


def solution(mesh):
    grid_size, orb_size = mesh.devices.shape
    z_size = min(8, grid_size // 2)
    split_mesh = Mesh(
        mesh.devices.reshape(grid_size // (2 * z_size), z_size, 2, orb_size), ("x", "z", "core", "orb")
    )
    placed = (P(GRID, None, None, "orb"), P(GRID, None, None))
    return jax.shard_map(
        on_device,
        mesh=split_mesh,
        in_specs=placed,
        out_specs=(P(GRID, None, None, "orb"), P("orb", GRID), P("orb", GRID)),
        check_vma=False,
    )
```

```python
import jax
import jax.numpy as jnp
from jax import lax
from jax.sharding import Mesh, PartitionSpec as P

DEGREE = 4
GRID = ("x", "z", "core")


STENCIL = (-205.0 / 72.0, 8.0 / 5.0, -1.0 / 5.0, 8.0 / 315.0, -1.0 / 560.0)
LOWER_EDGE = -2.0
CUT_EDGE = 1.5
UPPER_EDGE = 10.0
EPSILON = 1e-06


def halo_layers(shard, width):
    size = lax.axis_size(GRID)
    length = shard.shape[0]
    up = [(i, i + 1) for i in range(size - 1)]
    down = [(j, i) for i, j in up]
    last = lax.slice_in_dim(shard, length - width, length, axis=0).astype(jnp.bfloat16)
    initial = lax.slice_in_dim(shard, 0, width, axis=0).astype(jnp.bfloat16)
    before = lax.ppermute(last, GRID, up).astype(shard.dtype)
    after = lax.ppermute(initial, GRID, down).astype(shard.dtype)
    return jnp.concatenate([before, shard, after], axis=0)


def plane_matrix(rows_y, cols_x):
    flat_count = rows_y * cols_x
    index_all = jnp.arange(flat_count, dtype=jnp.int32)
    row_y = (index_all // cols_x)[:, None]
    row_x = (index_all % cols_x)[:, None]
    col_y = (index_all // cols_x)[None, :]
    col_x = (index_all % cols_x)[None, :]
    delta_y = jnp.mod(row_y - col_y, rows_y)
    delta_x = jnp.mod(row_x - col_x, cols_x)
    same_y = delta_y == 0
    same_x = delta_x == 0
    matrix = jnp.zeros((flat_count, flat_count), jnp.float32)
    for offset in range(1, 5):
        for signed in (offset, -offset):
            hit_y = jnp.logical_and(same_x, delta_y == signed % rows_y)
            hit_x = jnp.logical_and(same_y, delta_x == signed % cols_x)
            matrix = matrix + STENCIL[offset] * (
                hit_y.astype(jnp.float32) + hit_x.astype(jnp.float32)
            )
    return matrix


def apply_hamiltonian(current, potential, plane):
    layers, rows_y, cols_x, width = current.shape
    padded = halo_layers(current, 4)
    laplacian = 3.0 * STENCIL[0] * current
    for offset in range(1, 5):
        laplacian = laplacian + STENCIL[offset] * (
            padded[4 + offset : 4 + offset + layers] + padded[4 - offset : 4 - offset + layers]
        )
    flat = current.reshape(layers, rows_y * cols_x, width)
    in_plane = jnp.einsum(
        "pq,zqo->zpo",
        plane,
        flat,
        precision=lax.Precision.HIGH,
        preferred_element_type=jnp.float32,
    )
    laplacian = laplacian + in_plane.reshape(current.shape)
    return -0.5 * laplacian + potential[:, :, :, None] * current


def chebyshev(initial, potential, plane):
    half_width = (UPPER_EDGE - CUT_EDGE) / 2.0
    centre = (UPPER_EDGE + CUT_EDGE) / 2.0
    sigma_now = half_width / (LOWER_EDGE - centre)
    gamma_ratio = 2.0 / sigma_now
    previous = initial
    current = (
        sigma_now / half_width * (apply_hamiltonian(previous, potential, plane) - centre * previous)
    )
    for degree_step in range(DEGREE - 1):
        sigma_next = 1.0 / (gamma_ratio - sigma_now)
        following = (
            2.0
            * sigma_next
            / half_width
            * (apply_hamiltonian(current, potential, plane) - centre * current)
            - sigma_now * sigma_next * previous
        )
        previous, current, sigma_now = (current, following, sigma_next)
    return current


def contract_points(left_side, right_side):
    return lax.dot_general(
        left_side, right_side, (((0,), (0,)), ((), ())), preferred_element_type=jnp.float32
    )


def reduce_scatter_grid(slots):
    pairs = lax.axis_size("core")
    mine = lax.axis_index("core")
    split = slots.reshape((slots.shape[0] // pairs, pairs) + slots.shape[1:])
    low, high = split[:, 0], split[:, 1]
    keep = jnp.where(mine == 1, high, low)
    send = jnp.where(mine == 1, low, high)
    chip_part = keep + lax.ppermute(send, "core", [(0, 1), (1, 0)])
    chip_part = chip_part.reshape((lax.axis_size("x"), lax.axis_size("z")) + slots.shape[1:])
    row_part = jnp.sum(lax.all_to_all(chip_part, "x", 0, 0, tiled=True), axis=0)
    return jnp.sum(lax.all_to_all(row_part, "z", 0, 0, tiled=True), axis=0)


def gather_ring(block):
    size = lax.axis_size("orb")
    right = [(i, (i + 1) % size) for i in range(size)]
    left = [(i, (i - 1) % size) for i in range(size)]
    ahead = {0: block}
    from_left, from_right = block, block
    for step in range(1, size // 2 + 1):
        from_left = lax.ppermute(from_left, "orb", right)
        ahead[size - step] = from_left
        if step <= (size - 1) // 2:
            from_right = lax.ppermute(from_right, "orb", left)
            ahead[step] = from_right
    return [ahead[k] for k in range(size)]


def on_device(orbitals, potential):
    own_width = orbitals.shape[3]
    point_count = orbitals.shape[0] * orbitals.shape[1] * orbitals.shape[2]
    grid_size = lax.axis_size(GRID)
    point_total = float(point_count * grid_size)
    plane = plane_matrix(orbitals.shape[1], orbitals.shape[2])
    result_block = chebyshev(orbitals, potential, plane)
    own_squares = jnp.sum(result_block * result_block, axis=(0, 1, 2))
    rounded_orbitals = result_block.astype(jnp.bfloat16).reshape(point_count, own_width)
    rounded_image = (
        apply_hamiltonian(result_block, potential, plane)
        .astype(jnp.bfloat16)
        .reshape(point_count, own_width)
    )
    blocks = gather_ring(rounded_orbitals)
    total_width = own_width * len(blocks)
    rows = total_width // grid_size
    hamiltonian_part = jnp.concatenate(
        [contract_points(block, rounded_image) for block in blocks], axis=0
    )
    margin_part = jnp.concatenate(
        [contract_points(block, rounded_orbitals) for block in blocks], axis=0
    )
    column_squares = jnp.concatenate(
        [jnp.sum(jnp.square(block.astype(jnp.float32)), axis=0) for block in blocks], axis=0
    )
    body = jnp.concatenate(
        [
            hamiltonian_part.reshape(grid_size, rows, own_width),
            margin_part.reshape(grid_size, rows, own_width),
        ],
        axis=2,
    )
    tail = jnp.concatenate(
        [
            column_squares.reshape(grid_size, rows),
            jnp.broadcast_to(own_squares[None, :], (grid_size, own_width)),
            jnp.zeros((grid_size, own_width - rows), jnp.float32),
        ],
        axis=1,
    )
    slots = jnp.concatenate([body, tail[:, None, :]], axis=1)
    slots = jnp.roll(slots, lax.axis_index("orb") * (grid_size * own_width // total_width), axis=0)
    combined = reduce_scatter_grid(slots)
    scale_own = 1.0 / jnp.sqrt(combined[rows, rows : rows + own_width] / point_total + EPSILON)
    column_scale = 1.0 / jnp.sqrt(combined[rows, :rows] / point_total + EPSILON)
    filtered = result_block * scale_own
    pair_scale = scale_own[:, None] * column_scale[None, :] / point_total
    hamiltonian_block = combined[:rows, :own_width].T * pair_scale
    margin_block = combined[:rows, own_width:].T * pair_scale
    return (filtered, hamiltonian_block, margin_block)


def solution(mesh):
    grid_size, orb_size = mesh.devices.shape
    z_size = min(8, grid_size // 2)
    split_mesh = Mesh(
        mesh.devices.reshape(grid_size // (2 * z_size), z_size, 2, orb_size), ("x", "z", "core", "orb")
    )
    placed = (P(GRID, None, None, "orb"), P(GRID, None, None))
    return jax.shard_map(
        on_device,
        mesh=split_mesh,
        in_specs=placed,
        out_specs=(P(GRID, None, None, "orb"), P("orb", GRID), P("orb", GRID)),
        check_vma=False,
    )
```

```python
import jax
import jax.numpy as jnp
from jax import lax
from jax.sharding import Mesh, PartitionSpec as P

DEGREE = 4
GRID = ("x1", "x0", "z", "core")


STENCIL = (-205.0 / 72.0, 8.0 / 5.0, -1.0 / 5.0, 8.0 / 315.0, -1.0 / 560.0)
LOWER_EDGE = -2.0
CUT_EDGE = 1.5
UPPER_EDGE = 10.0
EPSILON = 1e-06


def halo_layers(shard, width):
    size = lax.axis_size(GRID)
    length = shard.shape[0]
    up = [(i, i + 1) for i in range(size - 1)]
    down = [(j, i) for i, j in up]
    last = lax.slice_in_dim(shard, length - width, length, axis=0).astype(jnp.bfloat16)
    initial = lax.slice_in_dim(shard, 0, width, axis=0).astype(jnp.bfloat16)
    before = lax.ppermute(last, GRID, up).astype(shard.dtype)
    after = lax.ppermute(initial, GRID, down).astype(shard.dtype)
    return jnp.concatenate([before, shard, after], axis=0)


def plane_matrix(rows_y, cols_x):
    flat_count = rows_y * cols_x
    index_all = jnp.arange(flat_count, dtype=jnp.int32)
    row_y = (index_all // cols_x)[:, None]
    row_x = (index_all % cols_x)[:, None]
    col_y = (index_all // cols_x)[None, :]
    col_x = (index_all % cols_x)[None, :]
    delta_y = jnp.mod(row_y - col_y, rows_y)
    delta_x = jnp.mod(row_x - col_x, cols_x)
    same_y = delta_y == 0
    same_x = delta_x == 0
    matrix = jnp.zeros((flat_count, flat_count), jnp.float32)
    for offset in range(1, 5):
        for signed in (offset, -offset):
            hit_y = jnp.logical_and(same_x, delta_y == signed % rows_y)
            hit_x = jnp.logical_and(same_y, delta_x == signed % cols_x)
            matrix = matrix + STENCIL[offset] * (
                hit_y.astype(jnp.float32) + hit_x.astype(jnp.float32)
            )
    return matrix


def apply_hamiltonian(current, potential, plane):
    layers, rows_y, cols_x, width = current.shape
    padded = halo_layers(current, 4)
    laplacian = 3.0 * STENCIL[0] * current
    for offset in range(1, 5):
        laplacian = laplacian + STENCIL[offset] * (
            padded[4 + offset : 4 + offset + layers] + padded[4 - offset : 4 - offset + layers]
        )
    flat = current.reshape(layers, rows_y * cols_x, width)
    in_plane = jnp.einsum(
        "pq,zqo->zpo",
        plane,
        flat,
        precision=lax.Precision.HIGH,
        preferred_element_type=jnp.float32,
    )
    laplacian = laplacian + in_plane.reshape(current.shape)
    return -0.5 * laplacian + potential[:, :, :, None] * current


def chebyshev(initial, potential, plane):
    half_width = (UPPER_EDGE - CUT_EDGE) / 2.0
    centre = (UPPER_EDGE + CUT_EDGE) / 2.0
    sigma_now = half_width / (LOWER_EDGE - centre)
    gamma_ratio = 2.0 / sigma_now
    previous = initial
    current = (
        sigma_now / half_width * (apply_hamiltonian(previous, potential, plane) - centre * previous)
    )
    for degree_step in range(DEGREE - 1):
        sigma_next = 1.0 / (gamma_ratio - sigma_now)
        following = (
            2.0
            * sigma_next
            / half_width
            * (apply_hamiltonian(current, potential, plane) - centre * current)
            - sigma_now * sigma_next * previous
        )
        previous, current, sigma_now = (current, following, sigma_next)
    return current


def contract_points(left_side, right_side):
    return lax.dot_general(
        left_side, right_side, (((0,), (0,)), ((), ())), preferred_element_type=jnp.float32
    )


def reduce_scatter_grid(slots):
    pairs = lax.axis_size("core")
    mine = lax.axis_index("core")
    split = slots.reshape((slots.shape[0] // pairs, pairs) + slots.shape[1:])
    low, high = split[:, 0], split[:, 1]
    keep = jnp.where(mine == 1, high, low)
    send = jnp.where(mine == 1, low, high)
    chip_part = keep + lax.ppermute(send, "core", [(0, 1), (1, 0)])
    halves = chip_part.reshape(
        (lax.axis_size("x1"), lax.axis_size("x0"), lax.axis_size("z")) + slots.shape[1:]
    )
    if lax.axis_size("x0") == 2:
        side = lax.axis_index("x0")
        low, high = halves[:, 0], halves[:, 1]
        keep = jnp.where(side == 1, high, low)
        send = jnp.where(side == 1, low, high)
        halves = keep + lax.ppermute(send, "x0", [(0, 1), (1, 0)])
    else:
        halves = halves[:, 0]
    received = lax.all_to_all(halves.reshape((-1,) + slots.shape[1:]), ("x1", "z"), 0, 0, tiled=True)
    return jnp.sum(received, axis=0)


def gather_ring(block):
    size = lax.axis_size("orb")
    right = [(i, (i + 1) % size) for i in range(size)]
    left = [(i, (i - 1) % size) for i in range(size)]
    ahead = {0: block}
    from_left, from_right = block, block
    for step in range(1, size // 2 + 1):
        from_left = lax.ppermute(from_left, "orb", right)
        ahead[size - step] = from_left
        if step <= (size - 1) // 2:
            from_right = lax.ppermute(from_right, "orb", left)
            ahead[step] = from_right
    return [ahead[k] for k in range(size)]


def on_device(orbitals, potential):
    own_width = orbitals.shape[3]
    point_count = orbitals.shape[0] * orbitals.shape[1] * orbitals.shape[2]
    grid_size = lax.axis_size(GRID)
    point_total = float(point_count * grid_size)
    plane = plane_matrix(orbitals.shape[1], orbitals.shape[2])
    result_block = chebyshev(orbitals, potential, plane)
    own_squares = jnp.sum(result_block * result_block, axis=(0, 1, 2))
    rounded_orbitals = result_block.astype(jnp.bfloat16).reshape(point_count, own_width)
    rounded_image = (
        apply_hamiltonian(result_block, potential, plane)
        .astype(jnp.bfloat16)
        .reshape(point_count, own_width)
    )
    blocks = gather_ring(rounded_orbitals)
    total_width = own_width * len(blocks)
    rows = total_width // grid_size
    hamiltonian_part = jnp.concatenate(
        [contract_points(block, rounded_image) for block in blocks], axis=0
    )
    margin_part = jnp.concatenate(
        [contract_points(block, rounded_orbitals) for block in blocks], axis=0
    )
    column_squares = jnp.concatenate(
        [jnp.sum(jnp.square(block.astype(jnp.float32)), axis=0) for block in blocks], axis=0
    )
    body = jnp.concatenate(
        [
            hamiltonian_part.reshape(grid_size, rows, own_width),
            margin_part.reshape(grid_size, rows, own_width),
        ],
        axis=2,
    )
    tail = jnp.concatenate(
        [
            column_squares.reshape(grid_size, rows),
            jnp.broadcast_to(own_squares[None, :], (grid_size, own_width)),
            jnp.zeros((grid_size, own_width - rows), jnp.float32),
        ],
        axis=1,
    )
    slots = jnp.concatenate([body, tail[:, None, :]], axis=1)
    slots = jnp.roll(slots, lax.axis_index("orb") * (grid_size * own_width // total_width), axis=0)
    combined = reduce_scatter_grid(slots)
    scale_own = 1.0 / jnp.sqrt(combined[rows, rows : rows + own_width] / point_total + EPSILON)
    column_scale = 1.0 / jnp.sqrt(combined[rows, :rows] / point_total + EPSILON)
    filtered = result_block * scale_own
    pair_scale = scale_own[:, None] * column_scale[None, :] / point_total
    hamiltonian_block = combined[:rows, :own_width].T * pair_scale
    margin_block = combined[:rows, own_width:].T * pair_scale
    return (filtered, hamiltonian_block, margin_block)


def solution(mesh):
    grid_size, orb_size = mesh.devices.shape
    z_size = min(8, grid_size // 2)
    x_size = grid_size // (2 * z_size)
    x_low = 2 if x_size % 2 == 0 else 1
    split_mesh = Mesh(
        mesh.devices.reshape(x_size // x_low, x_low, z_size, 2, orb_size),
        ("x1", "x0", "z", "core", "orb"),
    )
    placed = (P(GRID, None, None, "orb"), P(GRID, None, None))
    return jax.shard_map(
        on_device,
        mesh=split_mesh,
        in_specs=placed,
        out_specs=(P(GRID, None, None, "orb"), P("orb", GRID), P("orb", GRID)),
        check_vma=False,
    )
```

```python
import jax
import jax.numpy as jnp
from jax import lax
from jax.sharding import Mesh, PartitionSpec as P

DEGREE = 4
GRID = ("x", "z", "core")


STENCIL = (-205.0 / 72.0, 8.0 / 5.0, -1.0 / 5.0, 8.0 / 315.0, -1.0 / 560.0)
LOWER_EDGE = -2.0
CUT_EDGE = 1.5
UPPER_EDGE = 10.0
EPSILON = 1e-06


def halo_layers(shard, width):
    size = lax.axis_size(GRID)
    length = shard.shape[0]
    up = [(i, i + 1) for i in range(size - 1)]
    down = [(j, i) for i, j in up]
    last = lax.slice_in_dim(shard, length - width, length, axis=0).astype(jnp.bfloat16)
    initial = lax.slice_in_dim(shard, 0, width, axis=0).astype(jnp.bfloat16)
    before = lax.ppermute(last, GRID, up).astype(shard.dtype)
    after = lax.ppermute(initial, GRID, down).astype(shard.dtype)
    return jnp.concatenate([before, shard, after], axis=0)


def plane_matrix(rows_y, cols_x):
    flat_count = rows_y * cols_x
    index_all = jnp.arange(flat_count, dtype=jnp.int32)
    row_y = (index_all // cols_x)[:, None]
    row_x = (index_all % cols_x)[:, None]
    col_y = (index_all // cols_x)[None, :]
    col_x = (index_all % cols_x)[None, :]
    delta_y = jnp.mod(row_y - col_y, rows_y)
    delta_x = jnp.mod(row_x - col_x, cols_x)
    same_y = delta_y == 0
    same_x = delta_x == 0
    matrix = jnp.zeros((flat_count, flat_count), jnp.float32)
    for offset in range(1, 5):
        for signed in (offset, -offset):
            hit_y = jnp.logical_and(same_x, delta_y == signed % rows_y)
            hit_x = jnp.logical_and(same_y, delta_x == signed % cols_x)
            matrix = matrix + STENCIL[offset] * (
                hit_y.astype(jnp.float32) + hit_x.astype(jnp.float32)
            )
    return matrix


def apply_hamiltonian(current, potential, plane):
    layers, rows_y, cols_x, width = current.shape
    padded = halo_layers(current, 4)
    laplacian = 3.0 * STENCIL[0] * current
    for offset in range(1, 5):
        laplacian = laplacian + STENCIL[offset] * (
            padded[4 + offset : 4 + offset + layers] + padded[4 - offset : 4 - offset + layers]
        )
    flat = current.reshape(layers, rows_y * cols_x, width)
    in_plane = jnp.einsum(
        "pq,zqo->zpo",
        plane,
        flat,
        precision=lax.Precision.HIGH,
        preferred_element_type=jnp.float32,
    )
    laplacian = laplacian + in_plane.reshape(current.shape)
    return -0.5 * laplacian + potential[:, :, :, None] * current


def chebyshev(initial, potential, plane):
    half_width = (UPPER_EDGE - CUT_EDGE) / 2.0
    centre = (UPPER_EDGE + CUT_EDGE) / 2.0
    sigma_now = half_width / (LOWER_EDGE - centre)
    gamma_ratio = 2.0 / sigma_now
    previous = initial
    current = (
        sigma_now / half_width * (apply_hamiltonian(previous, potential, plane) - centre * previous)
    )
    for degree_step in range(DEGREE - 1):
        sigma_next = 1.0 / (gamma_ratio - sigma_now)
        following = (
            2.0
            * sigma_next
            / half_width
            * (apply_hamiltonian(current, potential, plane) - centre * current)
            - sigma_now * sigma_next * previous
        )
        previous, current, sigma_now = (current, following, sigma_next)
    return current


def contract_points(left_side, right_side):
    return lax.dot_general(
        left_side, right_side, (((0,), (0,)), ((), ())), preferred_element_type=jnp.float32
    )


def reduce_scatter_grid(slots):
    pairs = lax.axis_size("core")
    mine = lax.axis_index("core")
    split = slots.reshape((slots.shape[0] // pairs, pairs) + slots.shape[1:])
    low, high = split[:, 0], split[:, 1]
    keep = jnp.where(mine == 1, high, low)
    send = jnp.where(mine == 1, low, high)
    chip_part = keep + lax.ppermute(send, "core", [(0, 1), (1, 0)])
    chip_part = chip_part.reshape((lax.axis_size("x"), lax.axis_size("z")) + slots.shape[1:])
    row_part = jnp.sum(lax.all_to_all(chip_part, "x", 0, 0, tiled=True), axis=0)
    return jnp.sum(lax.all_to_all(row_part, "z", 0, 0, tiled=True), axis=0)


def gather_ring(block):
    size = lax.axis_size("orb")
    right = [(i, (i + 1) % size) for i in range(size)]
    left = [(i, (i - 1) % size) for i in range(size)]
    ahead = {0: block}
    from_left, from_right = block, block
    for step in range(1, size // 2 + 1):
        from_left = lax.ppermute(from_left, "orb", right)
        ahead[size - step] = from_left
        if step <= (size - 1) // 2:
            from_right = lax.ppermute(from_right, "orb", left)
            ahead[step] = from_right
    return [ahead[k] for k in range(size)]


def on_device(orbitals, potential):
    own_width = orbitals.shape[3]
    point_count = orbitals.shape[0] * orbitals.shape[1] * orbitals.shape[2]
    grid_size = lax.axis_size(GRID)
    point_total = float(point_count * grid_size)
    plane = plane_matrix(orbitals.shape[1], orbitals.shape[2])
    result_block = chebyshev(orbitals, potential, plane)
    own_squares = jnp.sum(result_block * result_block, axis=(0, 1, 2))
    rounded_orbitals = result_block.astype(jnp.bfloat16).reshape(point_count, own_width)
    rounded_image = (
        apply_hamiltonian(result_block, potential, plane)
        .astype(jnp.bfloat16)
        .reshape(point_count, own_width)
    )
    rounded_orbitals, rounded_image = lax.optimization_barrier((rounded_orbitals, rounded_image))
    blocks = gather_ring(rounded_orbitals)
    total_width = own_width * len(blocks)
    rows = total_width // grid_size
    hamiltonian_part = jnp.concatenate(
        [contract_points(block, rounded_image) for block in blocks], axis=0
    )
    margin_part = jnp.concatenate(
        [contract_points(block, rounded_orbitals) for block in blocks], axis=0
    )
    column_squares = jnp.concatenate(
        [jnp.sum(jnp.square(block.astype(jnp.float32)), axis=0) for block in blocks], axis=0
    )
    body = jnp.concatenate(
        [
            hamiltonian_part.reshape(grid_size, rows, own_width),
            margin_part.reshape(grid_size, rows, own_width),
        ],
        axis=2,
    )
    tail = jnp.concatenate(
        [
            column_squares.reshape(grid_size, rows),
            jnp.broadcast_to(own_squares[None, :], (grid_size, own_width)),
            jnp.zeros((grid_size, own_width - rows), jnp.float32),
        ],
        axis=1,
    )
    slots = jnp.concatenate([body, tail[:, None, :]], axis=1)
    slots = jnp.roll(slots, lax.axis_index("orb") * (grid_size * own_width // total_width), axis=0)
    combined = reduce_scatter_grid(slots)
    scale_own = 1.0 / jnp.sqrt(combined[rows, rows : rows + own_width] / point_total + EPSILON)
    column_scale = 1.0 / jnp.sqrt(combined[rows, :rows] / point_total + EPSILON)
    filtered = result_block * scale_own
    pair_scale = scale_own[:, None] * column_scale[None, :] / point_total
    hamiltonian_block = combined[:rows, :own_width].T * pair_scale
    margin_block = combined[:rows, own_width:].T * pair_scale
    return (filtered, hamiltonian_block, margin_block)


def solution(mesh):
    grid_size, orb_size = mesh.devices.shape
    z_size = min(8, grid_size // 2)
    split_mesh = Mesh(
        mesh.devices.reshape(grid_size // (2 * z_size), z_size, 2, orb_size), ("x", "z", "core", "orb")
    )
    placed = (P(GRID, None, None, "orb"), P(GRID, None, None))
    return jax.shard_map(
        on_device,
        mesh=split_mesh,
        in_specs=placed,
        out_specs=(P(GRID, None, None, "orb"), P("orb", GRID), P("orb", GRID)),
        check_vma=False,
    )
```

```python
import jax
import jax.numpy as jnp
from jax import lax
from jax.sharding import Mesh, PartitionSpec as P

DEGREE = 4
GRID = ("x", "z", "core")


STENCIL = (-205.0 / 72.0, 8.0 / 5.0, -1.0 / 5.0, 8.0 / 315.0, -1.0 / 560.0)
LOWER_EDGE = -2.0
CUT_EDGE = 1.5
UPPER_EDGE = 10.0
EPSILON = 1e-06


def halo_layers(shard, width):
    size = lax.axis_size(GRID)
    length = shard.shape[0]
    up = [(i, i + 1) for i in range(size - 1)]
    down = [(j, i) for i, j in up]
    last = lax.slice_in_dim(shard, length - width, length, axis=0).astype(jnp.bfloat16)
    initial = lax.slice_in_dim(shard, 0, width, axis=0).astype(jnp.bfloat16)
    before = lax.ppermute(last, GRID, up).astype(shard.dtype)
    after = lax.ppermute(initial, GRID, down).astype(shard.dtype)
    return jnp.concatenate([before, shard, after], axis=0)


def plane_matrix(rows_y, cols_x):
    flat_count = rows_y * cols_x
    index_all = jnp.arange(flat_count, dtype=jnp.int32)
    row_y = (index_all // cols_x)[:, None]
    row_x = (index_all % cols_x)[:, None]
    col_y = (index_all // cols_x)[None, :]
    col_x = (index_all % cols_x)[None, :]
    delta_y = jnp.mod(row_y - col_y, rows_y)
    delta_x = jnp.mod(row_x - col_x, cols_x)
    same_y = delta_y == 0
    same_x = delta_x == 0
    matrix = jnp.zeros((flat_count, flat_count), jnp.float32)
    for offset in range(1, 5):
        for signed in (offset, -offset):
            hit_y = jnp.logical_and(same_x, delta_y == signed % rows_y)
            hit_x = jnp.logical_and(same_y, delta_x == signed % cols_x)
            matrix = matrix + STENCIL[offset] * (
                hit_y.astype(jnp.float32) + hit_x.astype(jnp.float32)
            )
    return matrix


def apply_hamiltonian(current, potential, plane):
    layers, rows_y, cols_x, width = current.shape
    padded = halo_layers(current, 4)
    laplacian = 3.0 * STENCIL[0] * current
    for offset in range(1, 5):
        laplacian = laplacian + STENCIL[offset] * (
            padded[4 + offset : 4 + offset + layers] + padded[4 - offset : 4 - offset + layers]
        )
    flat = current.reshape(layers, rows_y * cols_x, width)
    in_plane = jnp.einsum(
        "pq,zqo->zpo",
        plane,
        flat,
        precision=lax.Precision.HIGH,
        preferred_element_type=jnp.float32,
    )
    laplacian = laplacian + in_plane.reshape(current.shape)
    return -0.5 * laplacian + potential[:, :, :, None] * current


def chebyshev(initial, potential, plane):
    half_width = (UPPER_EDGE - CUT_EDGE) / 2.0
    centre = (UPPER_EDGE + CUT_EDGE) / 2.0
    sigma_now = half_width / (LOWER_EDGE - centre)
    gamma_ratio = 2.0 / sigma_now
    previous = initial
    current = (
        sigma_now / half_width * (apply_hamiltonian(previous, potential, plane) - centre * previous)
    )
    for degree_step in range(DEGREE - 1):
        sigma_next = 1.0 / (gamma_ratio - sigma_now)
        following = (
            2.0
            * sigma_next
            / half_width
            * (apply_hamiltonian(current, potential, plane) - centre * current)
            - sigma_now * sigma_next * previous
        )
        previous, current, sigma_now = (current, following, sigma_next)
    return current


def contract_points(left_side, right_side):
    return lax.dot_general(
        left_side, right_side, (((0,), (0,)), ((), ())), preferred_element_type=jnp.float32
    )


def reduce_scatter_grid(slots):
    pairs = lax.axis_size("core")
    mine = lax.axis_index("core")
    split = slots.reshape((slots.shape[0] // pairs, pairs) + slots.shape[1:])
    low, high = split[:, 0], split[:, 1]
    keep = jnp.where(mine == 1, high, low)
    send = jnp.where(mine == 1, low, high)
    chip_part = keep + lax.ppermute(send, "core", [(0, 1), (1, 0)])
    chip_part = chip_part.reshape((lax.axis_size("x"), lax.axis_size("z")) + slots.shape[1:])
    row_part = jnp.sum(lax.all_to_all(chip_part, "x", 0, 0, tiled=True), axis=0)
    return jnp.sum(lax.all_to_all(row_part, "z", 0, 0, tiled=True), axis=0)


def gather_ring(block):
    size = lax.axis_size("orb")
    right = [(i, (i + 1) % size) for i in range(size)]
    left = [(i, (i - 1) % size) for i in range(size)]
    ahead = {0: block}
    from_left, from_right = block, block
    half = block.shape[0] // 2
    for step in range(1, size // 2 + 1):
        if step == size - step and size > 2:
            ahead[step] = jnp.concatenate(
                [
                    lax.ppermute(from_left[:half], "orb", right),
                    lax.ppermute(from_right[half:], "orb", left),
                ],
                axis=0,
            )
            continue
        from_left = lax.ppermute(from_left, "orb", right)
        ahead[size - step] = from_left
        if step <= (size - 1) // 2:
            from_right = lax.ppermute(from_right, "orb", left)
            ahead[step] = from_right
    return [ahead[k] for k in range(size)]


def on_device(orbitals, potential):
    own_width = orbitals.shape[3]
    point_count = orbitals.shape[0] * orbitals.shape[1] * orbitals.shape[2]
    grid_size = lax.axis_size(GRID)
    point_total = float(point_count * grid_size)
    plane = plane_matrix(orbitals.shape[1], orbitals.shape[2])
    result_block = chebyshev(orbitals, potential, plane)
    own_squares = jnp.sum(result_block * result_block, axis=(0, 1, 2))
    rounded_orbitals = result_block.astype(jnp.bfloat16).reshape(point_count, own_width)
    rounded_image = (
        apply_hamiltonian(result_block, potential, plane)
        .astype(jnp.bfloat16)
        .reshape(point_count, own_width)
    )
    blocks = gather_ring(rounded_orbitals)
    total_width = own_width * len(blocks)
    rows = total_width // grid_size
    hamiltonian_part = jnp.concatenate(
        [contract_points(block, rounded_image) for block in blocks], axis=0
    )
    margin_part = jnp.concatenate(
        [contract_points(block, rounded_orbitals) for block in blocks], axis=0
    )
    column_squares = jnp.concatenate(
        [jnp.sum(jnp.square(block.astype(jnp.float32)), axis=0) for block in blocks], axis=0
    )
    body = jnp.concatenate(
        [
            hamiltonian_part.reshape(grid_size, rows, own_width),
            margin_part.reshape(grid_size, rows, own_width),
        ],
        axis=2,
    )
    tail = jnp.concatenate(
        [
            column_squares.reshape(grid_size, rows),
            jnp.broadcast_to(own_squares[None, :], (grid_size, own_width)),
            jnp.zeros((grid_size, own_width - rows), jnp.float32),
        ],
        axis=1,
    )
    slots = jnp.concatenate([body, tail[:, None, :]], axis=1)
    slots = jnp.roll(slots, lax.axis_index("orb") * (grid_size * own_width // total_width), axis=0)
    combined = reduce_scatter_grid(slots)
    scale_own = 1.0 / jnp.sqrt(combined[rows, rows : rows + own_width] / point_total + EPSILON)
    column_scale = 1.0 / jnp.sqrt(combined[rows, :rows] / point_total + EPSILON)
    filtered = result_block * scale_own
    pair_scale = scale_own[:, None] * column_scale[None, :] / point_total
    hamiltonian_block = combined[:rows, :own_width].T * pair_scale
    margin_block = combined[:rows, own_width:].T * pair_scale
    return (filtered, hamiltonian_block, margin_block)


def solution(mesh):
    grid_size, orb_size = mesh.devices.shape
    z_size = min(8, grid_size // 2)
    split_mesh = Mesh(
        mesh.devices.reshape(grid_size // (2 * z_size), z_size, 2, orb_size), ("x", "z", "core", "orb")
    )
    placed = (P(GRID, None, None, "orb"), P(GRID, None, None))
    return jax.shard_map(
        on_device,
        mesh=split_mesh,
        in_specs=placed,
        out_specs=(P(GRID, None, None, "orb"), P("orb", GRID), P("orb", GRID)),
        check_vma=False,
    )
```

```python
import jax
import jax.numpy as jnp
from jax import lax
from jax.sharding import Mesh, PartitionSpec as P

DEGREE = 4
GRID = ("x", "z", "core")


STENCIL = (-205.0 / 72.0, 8.0 / 5.0, -1.0 / 5.0, 8.0 / 315.0, -1.0 / 560.0)
LOWER_EDGE = -2.0
CUT_EDGE = 1.5
UPPER_EDGE = 10.0
EPSILON = 1e-06


def halo_layers(shard, width):
    size = lax.axis_size(GRID)
    length = shard.shape[0]
    up = [(i, i + 1) for i in range(size - 1)]
    down = [(j, i) for i, j in up]
    last = lax.slice_in_dim(shard, length - width, length, axis=0).astype(jnp.bfloat16)
    initial = lax.slice_in_dim(shard, 0, width, axis=0).astype(jnp.bfloat16)
    before = lax.ppermute(last, GRID, up).astype(shard.dtype)
    after = lax.ppermute(initial, GRID, down).astype(shard.dtype)
    return jnp.concatenate([before, shard, after], axis=0)


def plane_matrix(rows_y, cols_x):
    flat_count = rows_y * cols_x
    index_all = jnp.arange(flat_count, dtype=jnp.int32)
    row_y = (index_all // cols_x)[:, None]
    row_x = (index_all % cols_x)[:, None]
    col_y = (index_all // cols_x)[None, :]
    col_x = (index_all % cols_x)[None, :]
    delta_y = jnp.mod(row_y - col_y, rows_y)
    delta_x = jnp.mod(row_x - col_x, cols_x)
    same_y = delta_y == 0
    same_x = delta_x == 0
    matrix = jnp.zeros((flat_count, flat_count), jnp.float32)
    for offset in range(1, 5):
        for signed in (offset, -offset):
            hit_y = jnp.logical_and(same_x, delta_y == signed % rows_y)
            hit_x = jnp.logical_and(same_y, delta_x == signed % cols_x)
            matrix = matrix + STENCIL[offset] * (
                hit_y.astype(jnp.float32) + hit_x.astype(jnp.float32)
            )
    return matrix


def apply_hamiltonian(current, potential, plane):
    layers, rows_y, cols_x, width = current.shape
    padded = halo_layers(current, 4)
    laplacian = 3.0 * STENCIL[0] * current
    for offset in range(1, 5):
        laplacian = laplacian + STENCIL[offset] * (
            padded[4 + offset : 4 + offset + layers] + padded[4 - offset : 4 - offset + layers]
        )
    flat = current.reshape(layers, rows_y * cols_x, width)
    in_plane = jnp.einsum(
        "pq,zqo->zpo",
        plane,
        flat,
        precision=lax.Precision.HIGH,
        preferred_element_type=jnp.float32,
    )
    laplacian = laplacian + in_plane.reshape(current.shape)
    return -0.5 * laplacian + potential[:, :, :, None] * current


def chebyshev(initial, potential, plane):
    half_width = (UPPER_EDGE - CUT_EDGE) / 2.0
    centre = (UPPER_EDGE + CUT_EDGE) / 2.0
    sigma_now = half_width / (LOWER_EDGE - centre)
    gamma_ratio = 2.0 / sigma_now
    previous = initial
    current = (
        sigma_now / half_width * (apply_hamiltonian(previous, potential, plane) - centre * previous)
    )
    for degree_step in range(DEGREE - 1):
        sigma_next = 1.0 / (gamma_ratio - sigma_now)
        following = (
            2.0
            * sigma_next
            / half_width
            * (apply_hamiltonian(current, potential, plane) - centre * current)
            - sigma_now * sigma_next * previous
        )
        previous, current, sigma_now = (current, following, sigma_next)
    return current


def contract_points(left_side, right_side):
    return lax.dot_general(
        left_side, right_side, (((0,), (0,)), ((), ())), preferred_element_type=jnp.float32
    )


def reduce_scatter_grid(slots):
    pairs = lax.axis_size("core")
    mine = lax.axis_index("core")
    split = slots.reshape((slots.shape[0] // pairs, pairs) + slots.shape[1:])
    low, high = split[:, 0], split[:, 1]
    keep = jnp.where(mine == 1, high, low)
    send = jnp.where(mine == 1, low, high)
    chip_part = keep + lax.ppermute(send, "core", [(0, 1), (1, 0)])
    received = lax.all_to_all(chip_part, ("x", "z"), 0, 0, tiled=True)
    return jnp.sum(received, axis=0)


def gather_ring(block):
    size = lax.axis_size("orb")
    right = [(i, (i + 1) % size) for i in range(size)]
    left = [(i, (i - 1) % size) for i in range(size)]
    ahead = {0: block}
    from_left, from_right = block, block
    half = block.shape[0] // 2
    for step in range(1, size // 2 + 1):
        if step == size - step and size > 2:
            ahead[step] = jnp.concatenate(
                [
                    lax.ppermute(from_left[:half], "orb", right),
                    lax.ppermute(from_right[half:], "orb", left),
                ],
                axis=0,
            )
            continue
        from_left = lax.ppermute(from_left, "orb", right)
        ahead[size - step] = from_left
        if step <= (size - 1) // 2:
            from_right = lax.ppermute(from_right, "orb", left)
            ahead[step] = from_right
    return [ahead[k] for k in range(size)]


def on_device(orbitals, potential):
    own_width = orbitals.shape[3]
    point_count = orbitals.shape[0] * orbitals.shape[1] * orbitals.shape[2]
    grid_size = lax.axis_size(GRID)
    point_total = float(point_count * grid_size)
    plane = plane_matrix(orbitals.shape[1], orbitals.shape[2])
    result_block = chebyshev(orbitals, potential, plane)
    own_squares = jnp.sum(result_block * result_block, axis=(0, 1, 2))
    rounded_orbitals = result_block.astype(jnp.bfloat16).reshape(point_count, own_width)
    rounded_image = (
        apply_hamiltonian(result_block, potential, plane)
        .astype(jnp.bfloat16)
        .reshape(point_count, own_width)
    )
    blocks = gather_ring(rounded_orbitals)
    total_width = own_width * len(blocks)
    rows = total_width // grid_size
    hamiltonian_part = jnp.concatenate(
        [contract_points(block, rounded_image) for block in blocks], axis=0
    )
    margin_part = jnp.concatenate(
        [contract_points(block, rounded_orbitals) for block in blocks], axis=0
    )
    column_squares = jnp.concatenate(
        [jnp.sum(jnp.square(block.astype(jnp.float32)), axis=0) for block in blocks], axis=0
    )
    body = jnp.concatenate(
        [
            hamiltonian_part.reshape(grid_size, rows, own_width),
            margin_part.reshape(grid_size, rows, own_width),
        ],
        axis=2,
    )
    tail = jnp.concatenate(
        [
            column_squares.reshape(grid_size, rows),
            jnp.broadcast_to(own_squares[None, :], (grid_size, own_width)),
            jnp.zeros((grid_size, own_width - rows), jnp.float32),
        ],
        axis=1,
    )
    slots = jnp.concatenate([body, tail[:, None, :]], axis=1)
    slots = jnp.roll(slots, lax.axis_index("orb") * (grid_size * own_width // total_width), axis=0)
    combined = reduce_scatter_grid(slots)
    scale_own = 1.0 / jnp.sqrt(combined[rows, rows : rows + own_width] / point_total + EPSILON)
    column_scale = 1.0 / jnp.sqrt(combined[rows, :rows] / point_total + EPSILON)
    filtered = result_block * scale_own
    pair_scale = scale_own[:, None] * column_scale[None, :] / point_total
    hamiltonian_block = combined[:rows, :own_width].T * pair_scale
    margin_block = combined[:rows, own_width:].T * pair_scale
    return (filtered, hamiltonian_block, margin_block)


def solution(mesh):
    grid_size, orb_size = mesh.devices.shape
    z_size = min(8, grid_size // 2)
    split_mesh = Mesh(
        mesh.devices.reshape(grid_size // (2 * z_size), z_size, 2, orb_size), ("x", "z", "core", "orb")
    )
    placed = (P(GRID, None, None, "orb"), P(GRID, None, None))
    return jax.shard_map(
        on_device,
        mesh=split_mesh,
        in_specs=placed,
        out_specs=(P(GRID, None, None, "orb"), P("orb", GRID), P("orb", GRID)),
        check_vma=False,
    )
```
